32 devices in a mesh: lat: 4 (over y, x), lon: 8 (over z, core).
Axes of the slice: x: 2, y: 2, z: 4, core: 2. Of those that a mesh axis runs over, the one named last changes fastest.
Arguments:
- swath_input: bfloat16 [64, 64, 64, 256], P(('lat', 'lon')), may hold values from -6 to 6
- conv_weight: bfloat16 [3, 3, 256, 256], replicated, may hold values from -0.125 to 0.125
- conv_bias: float32 [256], replicated, may hold values from -3 to 3
- block_band: int32 [64, 1], P(('lat', 'lon')), may hold values from 0 to 3, as said below
- row_offset: int32 [64], P(('lat', 'lon')), may hold values from 0 to 8
- col_offset: int32 [64], P(('lat', 'lon')), may hold values from 0 to 8
- row_weights: bfloat16 [64, 16, 32], P(('lat', 'lon')), may hold values from -1 to 1
- col_weights: bfloat16 [64, 16, 32], P(('lat', 'lon')), may hold values from -1 to 1
- background: bfloat16 [96, 192, 256], P('lat', 'lon'), may hold values from -6 to 6
- depth_weight: float32 [2, 7, 7, 256], replicated, may hold values from -0.875 to 0.875
- norm_gain: float32 [2, 256], replicated, may hold values from 0.1 to 1.9
- up_weight: bfloat16 [2, 256, 1024], replicated, may hold values from -0.375 to 0.375
- down_weight: bfloat16 [2, 1024, 256], replicated, may hold values from -0.1875 to 0.1875
Outputs:
- weather_grid: bfloat16 [96, 192, 256], P('lat', 'lon')
The draws below stay inside these ranges and needn't reach their ends.
Inputs may be any that keep to these rules, and one draw needn't show every extreme that they name: `block_band`: block b's band is the latitude band (b // 2) // 8 of the device that holds it, or one next to it; every device sends at least one block to a neighbouring band, at most 2 to each, and some device sends exactly 2 to one.
All inputs are finite; a program needn't handle non-finite values.
Results may differ from the reference program's by a relative error of at most 0.011.
Values may be sent and summed in bfloat16 or wider, within the bound.
No kernel may reach another device: no remote copies, remote signals or barrier semaphores. Data moves between devices by JAX's collectives and lax.ppermute only.
A program may use at most 64 MiB of HBM per device.

```python
import jax
import jax.numpy as jnp
from jax import lax

C = 256
HID = 1024
KS = 7
HALO = 3
LAYERS = 2
NB = 2
OBH = 32
OBW = 32
IBH = 64
IBW = 64
RB = 16
RW = 16
TH = 24
TW = 24
BANDS = 4
TILES_LON = 8
BLOCKS = 64
GH = 96
GW = 192
N_LON = 8


def draw_block_band(key, part):
    device_count = BLOCKS // NB
    device_ids = jnp.arange(device_count, dtype=jnp.int32)
    own_band = (device_ids // TILES_LON).astype(jnp.int32)
    key_side = jax.random.fold_in(key, 11)
    key_second = jax.random.fold_in(key, 23)
    side = (jax.random.randint(key_side, (device_count,), 0, 2).astype(jnp.int32) * 2 - 1).astype(jnp.int32)
    side = jnp.where(own_band == 0, 1, jnp.where(own_band == BANDS - 1, -1, side)).astype(jnp.int32)
    second = jax.random.randint(key_second, (device_count,), -1, 2).astype(jnp.int32)
    second = jnp.where(device_ids == 0, side, second).astype(jnp.int32)
    landing = own_band + second
    second = jnp.where((landing >= 0) & (landing < BANDS), second, 0).astype(jnp.int32)
    first_band = own_band + side
    second_band = own_band + second
    bands = jnp.stack([first_band, second_band], axis=1)
    return bands.reshape(BLOCKS, 1).astype(jnp.int32)


def plant(values, stream_key, smallest, high):
    place = [jax.random.randint(jax.random.fold_in(stream_key, axis), (), 0, length) for axis, length in enumerate(values.shape)]
    main_axis = values.shape.index(max(values.shape))
    beside = place[:main_axis] + [(place[main_axis] + 1) % values.shape[main_axis]] + place[main_axis + 1:]
    return values.at[tuple(place)].set(smallest).at[tuple(beside)].set(high)


def shard_levels(key, shape, shards, smallest, largest):
    level, own = 1.0, jax.random.fold_in(key, 6)
    for axis_at, blocks in shards:
        heights = jnp.exp(jax.random.uniform(jax.random.fold_in(own, axis_at), (blocks,), jnp.float32, smallest / len(shards), largest / len(shards)))
        level = level * jnp.repeat(heights, shape[axis_at] // blocks).reshape([-1 if axis == axis_at else 1 for axis in range(len(shape))])
    return level


def scatter_about(own_key, shape, deviation, bound, cuts=(), held_as=jnp.bfloat16):
    loudness = shard_levels(own_key, shape, cuts, -0.22, 0.18) if cuts else 1.0
    entries = jax.random.normal(own_key, shape, jnp.float32) * deviation * loudness
    return jnp.minimum(jnp.maximum(entries, -bound), bound).astype(held_as)


def setup_inputs(seed: int = 0) -> dict:
    seeds = jax.random.split(jax.random.key(seed), 14)
    return {
        "swath_input": scatter_about(seeds[0], (BLOCKS, IBH, IBW, C), 1.0, 6.0, ((0, 32),)),
        "conv_weight": scatter_about(seeds[1], (3, 3, C, C), (9 * C) ** -0.5, 0.125),
        "conv_bias": scatter_about(seeds[2], (C,), 0.5, 3.0, (), jnp.float32),
        "block_band": draw_block_band(jax.random.fold_in(seeds[13], 71), 0),
        "row_offset": plant(jax.random.randint(seeds[4], (BLOCKS,), 0, TH - RB + 1), jax.random.fold_in(seeds[4], 1), 0, TH - RB).astype(jnp.int32),
        "col_offset": plant(jax.random.randint(seeds[5], (BLOCKS,), 0, TW - RW + 1), jax.random.fold_in(seeds[5], 1), 0, TW - RW).astype(jnp.int32),
        "row_weights": scatter_about(seeds[6], (BLOCKS, RB, OBH), OBH ** -0.5, 1.0, ((0, 32),)),
        "col_weights": scatter_about(seeds[7], (BLOCKS, RW, OBW), OBW ** -0.5, 1.0, ((0, 32),)),
        "background": scatter_about(seeds[8], (GH, GW, C), 1.0, 6.0, ((0, 4), (1, 8))),
        "depth_weight": scatter_about(seeds[9], (LAYERS, KS, KS, C), (KS * KS) ** -0.5, 0.875, (), jnp.float32),
        "norm_gain": jnp.clip(1.0 + 0.18 * jax.random.normal(seeds[10], (LAYERS, C), jnp.float32), 0.1, 1.9),
        "up_weight": scatter_about(seeds[11], (LAYERS, C, HID), C ** -0.5, 0.375),
        "down_weight": scatter_about(seeds[12], (LAYERS, HID, C), HID ** -0.5, 0.1875),
    }


def resample_group(swath_group, conv_weight, conv_bias, row_group, col_group):
    convolved = lax.conv_general_dilated(swath_group.astype(jnp.float32), conv_weight.astype(jnp.float32), (2, 2), ((1, 1), (1, 1)), dimension_numbers=('NHWC', 'HWIO', 'NHWC'), precision=lax.Precision.HIGHEST)
    features = jax.nn.gelu(convolved + conv_bias).astype(jnp.bfloat16)
    row_mixed = jnp.einsum('nri,nijc->nrjc', row_group.astype(jnp.float32), features.astype(jnp.float32), precision=lax.Precision.HIGHEST)
    both_mixed = jnp.einsum('nrjc,nuj->nruc', row_mixed, col_group.astype(jnp.float32), precision=lax.Precision.HIGHEST)
    return both_mixed.astype(jnp.bfloat16)

def layer_apply(padded, depth_kernel, gain, up_matrix, down_matrix):
    height = padded.shape[0] - (KS - 1)
    width = padded.shape[1] - (KS - 1)
    channels = padded.shape[2]
    widened = padded.astype(jnp.float32)
    kernel = depth_kernel.reshape(KS, KS, 1, channels).astype(jnp.float32)
    mixed = lax.conv_general_dilated(widened[None], kernel, (1, 1), ((0, 0), (0, 0)), dimension_numbers=('NHWC', 'HWIO', 'NHWC'), feature_group_count=channels, precision=lax.Precision.HIGHEST)[0]
    centered = mixed - lax.optimization_barrier(jnp.mean(mixed, axis=-1, keepdims=True))
    variance = lax.optimization_barrier(jnp.mean(centered * centered, axis=-1, keepdims=True))
    normed = (centered * lax.rsqrt(variance + 1e-06) * gain).astype(jnp.bfloat16)
    flat_cells = normed.reshape(height * width, -1)
    hidden = jax.nn.gelu(jnp.dot(flat_cells, up_matrix, preferred_element_type=jnp.float32)).astype(jnp.bfloat16)
    output = jnp.dot(hidden, down_matrix, preferred_element_type=jnp.float32).reshape(height, width, -1)
    residual_part = widened[HALO:HALO + height, HALO:HALO + width]
    return (residual_part + output).astype(jnp.bfloat16)

def reference(swath_input, conv_weight, conv_bias, block_band, row_offset, col_offset, row_weights, col_weights, background, depth_weight, norm_gain, up_weight, down_weight):
    group_count = BLOCKS // NB
    swath_groups = swath_input.reshape(group_count, NB, IBH, IBW, C)
    row_groups = row_weights.reshape(group_count, NB, RB, OBH)
    col_groups = col_weights.reshape(group_count, NB, RW, OBW)
    resampled = lax.map(lambda packed: resample_group(packed[0], conv_weight, conv_bias, packed[1], packed[2]), (swath_groups, row_groups, col_groups))
    resampled = resampled.reshape(BLOCKS, RB, RW, C)
    block_index = jnp.arange(BLOCKS, dtype=jnp.int32)
    lon_tile = (block_index // NB % N_LON).astype(jnp.int32)
    row_start = (block_band[:, 0] * TH + row_offset).astype(jnp.int32)
    col_start = (lon_tile * TW + col_offset).astype(jnp.int32)

    def add_block(index, total):
        piece = resampled[index].astype(total.dtype)
        anchor = (row_start[index].astype(jnp.int32), col_start[index].astype(jnp.int32), jnp.zeros((), jnp.int32))
        current = lax.dynamic_slice(total, anchor, (RB, RW, C))
        return lax.dynamic_update_slice(total, current + piece, anchor)
    summed = lax.fori_loop(0, BLOCKS, add_block, jnp.zeros((GH, GW, C), jnp.float32))
    state = (background.astype(jnp.float32) + summed).astype(jnp.bfloat16)
    for layer_index in range(LAYERS):
        padded = jnp.pad(state, ((HALO, HALO), (0, 0), (0, 0)))
        padded = jnp.concatenate([padded[:, GW - HALO:], padded, padded[:, :HALO]], axis=1)
        state = layer_apply(padded, depth_weight[layer_index], norm_gain[layer_index], up_weight[layer_index], down_weight[layer_index])
    return state
```

```python
import jax
import jax.numpy as jnp
from jax import lax
from jax.sharding import PartitionSpec as P

KS = 7
HALO = 3
LAYERS = 2
CAP = 2
RB = 16
RW = 16


def shifted(value, axis, steps):
    count = lax.axis_size(axis)
    leading, last = (max(0, -steps), min(count, count - steps))
    return lax.ppermute(value, axis, [(source, source + steps) for source in range(leading, last)])


def with_halo(value, sides, width, wrap):
    for axis, dim in sides:
        size, length = (lax.axis_size(axis), value.shape[dim])
        up = [(i, (i + 1) % size) for i in range(size if wrap else size - 1)]
        down = [(j, i) for i, j in up]
        last = lax.slice_in_dim(value, length - width, length, axis=dim)
        leading = lax.slice_in_dim(value, 0, width, axis=dim)
        before = lax.ppermute(last, axis, up)
        after = lax.ppermute(leading, axis, down)
        value = jnp.concatenate([before, value, after], axis=dim)
    return value


def resample_local(blocks, row_mix, col_mix):
    row_mixed = jnp.einsum("nri,nijc->nrjc", row_mix, blocks, preferred_element_type=jnp.float32)
    both_mixed = jnp.einsum(
        "nrjc,nuj->nruc", row_mixed, col_mix.astype(jnp.float32), precision=lax.Precision.HIGHEST
    )
    return both_mixed.astype(jnp.bfloat16)


def place_rows(onehot, values):
    flat_values = values.reshape(values.shape[0], -1)
    placed = jnp.dot(onehot.astype(values.dtype), flat_values, preferred_element_type=jnp.float32)
    return placed.astype(values.dtype).reshape((onehot.shape[0],) + values.shape[1:])


def place_ints(onehot, values):
    return jnp.sum(jnp.where(onehot, values[None, :], 0), axis=1)


def keep_local(keep, values):
    shaped = keep.reshape((keep.shape[0],) + (1,) * (values.ndim - 1))
    return jnp.where(shaped, values, jnp.zeros_like(values))


def depthwise(widened, depth_kernel, height, width):
    mixed = None
    for e in range(KS):
        column = widened[:, e : e + width]
        for a in range(KS):
            term = column[a : a + height] * depth_kernel[a, e]
            mixed = term if mixed is None else mixed + term
    return mixed


def layer_apply(padded, depth_kernel, gain, up_matrix, down_matrix):
    height = padded.shape[0] - (KS - 1)
    width = padded.shape[1] - (KS - 1)
    widened = padded.astype(jnp.float32)
    mixed = depthwise(widened, depth_kernel, height, width)
    centered = mixed - jnp.mean(mixed, axis=-1, keepdims=True)
    variance = jnp.mean(centered * centered, axis=-1, keepdims=True)
    normed = (centered * lax.rsqrt(variance + 1e-06) * gain).astype(jnp.bfloat16)
    flat_cells = normed.reshape(height * width, -1)
    hidden = jax.nn.gelu(jnp.dot(flat_cells, up_matrix, preferred_element_type=jnp.float32)).astype(
        jnp.bfloat16
    )
    output = jnp.dot(hidden, down_matrix, preferred_element_type=jnp.float32).reshape(
        height, width, -1
    )
    residual_part = widened[HALO : HALO + height, HALO : HALO + width]
    return (residual_part + output).astype(jnp.bfloat16)


def per_device(
    swath_input,
    conv_weight,
    conv_bias,
    block_band,
    row_offset,
    col_offset,
    row_weights,
    col_weights,
    background,
    depth_weight,
    norm_gain,
    up_weight,
    down_weight,
):
    blocks_here = swath_input.shape[0]
    tile_rows = background.shape[0]
    tile_cols = background.shape[1]
    channels = background.shape[2]
    bands = lax.axis_size("lat")
    convolved = lax.conv_general_dilated(
        swath_input,
        conv_weight,
        (2, 2),
        ((1, 1), (1, 1)),
        dimension_numbers=("NHWC", "HWIO", "NHWC"),
        preferred_element_type=jnp.float32,
    )
    features = jax.nn.gelu(convolved + conv_bias).astype(jnp.bfloat16)
    resampled = resample_local(features, row_weights, col_weights)
    own_band = lax.axis_index("lat")
    offset_band = block_band[:, 0] - own_band
    staying = offset_band == 0
    positions = jnp.arange(blocks_here, dtype=jnp.int32)
    row_list = [row_offset]
    col_list = [col_offset]
    block_list = [keep_local(staying, resampled)]
    for step in (1, -1):
        going = offset_band == step
        earlier = jnp.sum(going[None, :] & (positions[None, :] < positions[:, None]), axis=1)
        table = (jnp.arange(CAP, dtype=jnp.int32)[:, None] == earlier[None, :]) & going[None, :]
        sent_blocks = place_rows(table, resampled)
        sent_rows = place_ints(table, row_offset)
        sent_cols = place_ints(table, col_offset)
        lane = jnp.arange(channels, dtype=jnp.int32)[None, :]
        header = jnp.where(
            lane == 0, sent_rows[:, None], jnp.where(lane == 1, sent_cols[:, None], 0)
        ).astype(jnp.bfloat16)
        header = jnp.broadcast_to(header[:, None, None, :], (CAP, 1, RW, channels))
        payload = jnp.concatenate([sent_blocks, header], axis=1)
        got = shifted(payload, "lat", step)
        block_list.append(got[:, :RB])
        got_header = got[:, RB, 0, :].astype(jnp.int32)
        row_list.append(got_header[:, 0])
        col_list.append(got_header[:, 1])
    arrived = jnp.concatenate(block_list, axis=0)
    all_rows = jnp.concatenate(row_list, axis=0)
    all_cols = jnp.concatenate(col_list, axis=0)
    row_place = (
        jnp.arange(tile_rows, dtype=jnp.int32)[None, :, None]
        == all_rows[:, None, None] + jnp.arange(RB, dtype=jnp.int32)[None, None, :]
    ).astype(jnp.bfloat16)
    col_place = (
        jnp.arange(tile_cols, dtype=jnp.int32)[None, :, None]
        == all_cols[:, None, None] + jnp.arange(RW, dtype=jnp.int32)[None, None, :]
    ).astype(jnp.bfloat16)
    lifted = jnp.einsum(
        "shr,sruc->shuc", row_place, arrived, preferred_element_type=jnp.float32
    ).astype(jnp.bfloat16)
    summed = jnp.einsum("swu,shuc->hwc", col_place, lifted, preferred_element_type=jnp.float32)
    state = (background.astype(jnp.float32) + summed).astype(jnp.bfloat16)
    reach = HALO * LAYERS
    widened = with_halo(state, (("lon", 1),), reach, True)
    widened = with_halo(widened, (("lat", 0),), reach, False)
    first_row = own_band * tile_rows
    for layer_index in range(LAYERS):
        widened = layer_apply(
            widened,
            depth_weight[layer_index],
            norm_gain[layer_index],
            up_weight[layer_index],
            down_weight[layer_index],
        )
        margin = (widened.shape[0] - tile_rows) // 2
        if margin:
            grid_row = first_row - margin + jnp.arange(widened.shape[0], dtype=jnp.int32)
            inside = (grid_row >= 0) & (grid_row < bands * tile_rows)
            widened = jnp.where(inside[:, None, None], widened, jnp.zeros_like(widened))
    return widened


def solution(mesh):
    in_specs = (
        P(("lat", "lon"), None, None, None),
        P(),
        P(),
        P(("lat", "lon"), None),
        P(("lat", "lon")),
        P(("lat", "lon")),
        P(("lat", "lon"), None, None),
        P(("lat", "lon"), None, None),
        P("lat", "lon", None),
        P(),
        P(),
        P(),
        P(),
    )
    out_specs = P("lat", "lon", None)
    return jax.shard_map(
        per_device, mesh=mesh, in_specs=in_specs, out_specs=out_specs, check_vma=False
    )
```

```python
import jax
import jax.numpy as jnp
from jax import lax
from jax.sharding import PartitionSpec as P

KS = 7
HALO = 3
LAYERS = 2
CAP = 2
RB = 16
RW = 16


def shifted(value, axis, steps):
    count = lax.axis_size(axis)
    leading, last = (max(0, -steps), min(count, count - steps))
    return lax.ppermute(value, axis, [(source, source + steps) for source in range(leading, last)])


def halo_all(value, reach):
    bands, tiles = lax.axis_size("lat"), lax.axis_size("lon")

    def send(piece, dlat, dlon):
        pairs = []
        for lat in range(bands):
            if 0 <= lat + dlat < bands:
                for lon in range(tiles):
                    pairs.append((lat * tiles + lon, (lat + dlat) * tiles + (lon + dlon) % tiles))
        return lax.ppermute(piece, ("lat", "lon"), pairs)

    top, bottom = value[:reach], value[-reach:]
    north = send(bottom, 1, 0)
    south = send(top, -1, 0)
    west = send(value[:, -reach:], 0, 1)
    east = send(value[:, :reach], 0, -1)
    north_west = send(bottom[:, -reach:], 1, 1)
    north_east = send(bottom[:, :reach], 1, -1)
    south_west = send(top[:, -reach:], -1, 1)
    south_east = send(top[:, :reach], -1, -1)
    upper = jnp.concatenate([north_west, north, north_east], axis=1)
    middle = jnp.concatenate([west, value, east], axis=1)
    lower = jnp.concatenate([south_west, south, south_east], axis=1)
    return jnp.concatenate([upper, middle, lower], axis=0)


def resample_local(blocks, row_mix, col_mix):
    row_mixed = jnp.einsum("nri,nijc->nrjc", row_mix, blocks, preferred_element_type=jnp.float32)
    both_mixed = jnp.einsum(
        "nrjc,nuj->nruc", row_mixed, col_mix.astype(jnp.float32), precision=lax.Precision.HIGHEST
    )
    return both_mixed.astype(jnp.bfloat16)


def place_rows(onehot, values):
    flat_values = values.reshape(values.shape[0], -1)
    placed = jnp.dot(onehot.astype(values.dtype), flat_values, preferred_element_type=jnp.float32)
    return placed.astype(values.dtype).reshape((onehot.shape[0],) + values.shape[1:])


def place_ints(onehot, values):
    return jnp.sum(jnp.where(onehot, values[None, :], 0), axis=1)


def keep_local(keep, values):
    shaped = keep.reshape((keep.shape[0],) + (1,) * (values.ndim - 1))
    return jnp.where(shaped, values, jnp.zeros_like(values))


def depthwise(widened, depth_kernel, height, width):
    mixed = None
    for e in range(KS):
        column = widened[:, e : e + width]
        for a in range(KS):
            term = column[a : a + height] * depth_kernel[a, e]
            mixed = term if mixed is None else mixed + term
    return mixed


def layer_apply(padded, depth_kernel, gain, up_matrix, down_matrix):
    height = padded.shape[0] - (KS - 1)
    width = padded.shape[1] - (KS - 1)
    spare = -width % 8
    widened = padded.astype(jnp.float32)
    if spare:
        widened = jnp.pad(widened, ((0, 0), (0, spare), (0, 0)))
    mixed = depthwise(widened, depth_kernel, height, width + spare)
    centered = mixed - jnp.mean(mixed, axis=-1, keepdims=True)
    variance = jnp.mean(centered * centered, axis=-1, keepdims=True)
    normed = (centered * lax.rsqrt(variance + 1e-06) * gain).astype(jnp.bfloat16)
    flat_cells = normed.reshape(height * (width + spare), -1)
    hidden = jax.nn.gelu(jnp.dot(flat_cells, up_matrix, preferred_element_type=jnp.float32)).astype(
        jnp.bfloat16
    )
    output = jnp.dot(hidden, down_matrix, preferred_element_type=jnp.float32).reshape(
        height, width + spare, -1
    )
    residual_part = widened[HALO : HALO + height, HALO : HALO + width + spare]
    return (residual_part + output).astype(jnp.bfloat16)[:, :width]


def per_device(
    swath_input,
    conv_weight,
    conv_bias,
    block_band,
    row_offset,
    col_offset,
    row_weights,
    col_weights,
    background,
    depth_weight,
    norm_gain,
    up_weight,
    down_weight,
):
    blocks_here = swath_input.shape[0]
    tile_rows = background.shape[0]
    tile_cols = background.shape[1]
    channels = background.shape[2]
    bands = lax.axis_size("lat")
    convolved = lax.conv_general_dilated(
        swath_input,
        conv_weight,
        (2, 2),
        ((1, 1), (1, 1)),
        dimension_numbers=("NHWC", "HWIO", "NHWC"),
        preferred_element_type=jnp.float32,
    )
    features = jax.nn.gelu(convolved + conv_bias).astype(jnp.bfloat16)
    resampled = resample_local(features, row_weights, col_weights)
    own_band = lax.axis_index("lat")
    offset_band = block_band[:, 0] - own_band
    staying = offset_band == 0
    positions = jnp.arange(blocks_here, dtype=jnp.int32)
    row_list = [row_offset]
    col_list = [col_offset]
    block_list = [keep_local(staying, resampled)]
    for step in (1, -1):
        going = offset_band == step
        earlier = jnp.sum(going[None, :] & (positions[None, :] < positions[:, None]), axis=1)
        table = (jnp.arange(CAP, dtype=jnp.int32)[:, None] == earlier[None, :]) & going[None, :]
        sent_blocks = place_rows(table, resampled)
        sent_rows = place_ints(table, row_offset)
        sent_cols = place_ints(table, col_offset)
        lane = jnp.arange(channels, dtype=jnp.int32)[None, :]
        header = jnp.where(
            lane == 0, sent_rows[:, None], jnp.where(lane == 1, sent_cols[:, None], 0)
        ).astype(jnp.bfloat16)
        header = jnp.broadcast_to(header[:, None, None, :], (CAP, 1, RW, channels))
        payload = jnp.concatenate([sent_blocks, header], axis=1)
        got = shifted(payload, "lat", step)
        block_list.append(got[:, :RB])
        got_header = got[:, RB, 0, :].astype(jnp.int32)
        row_list.append(got_header[:, 0])
        col_list.append(got_header[:, 1])
    arrived = jnp.concatenate(block_list, axis=0)
    all_rows = jnp.concatenate(row_list, axis=0)
    all_cols = jnp.concatenate(col_list, axis=0)
    row_place = (
        jnp.arange(tile_rows, dtype=jnp.int32)[None, :, None]
        == all_rows[:, None, None] + jnp.arange(RB, dtype=jnp.int32)[None, None, :]
    ).astype(jnp.bfloat16)
    col_place = (
        jnp.arange(tile_cols, dtype=jnp.int32)[None, :, None]
        == all_cols[:, None, None] + jnp.arange(RW, dtype=jnp.int32)[None, None, :]
    ).astype(jnp.bfloat16)
    lifted = jnp.einsum(
        "shr,sruc->shuc", row_place, arrived, preferred_element_type=jnp.float32
    ).astype(jnp.bfloat16)
    summed = jnp.einsum("swu,shuc->hwc", col_place, lifted, preferred_element_type=jnp.float32)
    state = (background.astype(jnp.float32) + summed).astype(jnp.bfloat16)
    reach = HALO * LAYERS
    widened = halo_all(state, reach)
    first_row = own_band * tile_rows
    for layer_index in range(LAYERS):
        widened = layer_apply(
            widened,
            depth_weight[layer_index],
            norm_gain[layer_index],
            up_weight[layer_index],
            down_weight[layer_index],
        )
        margin = (widened.shape[0] - tile_rows) // 2
        if margin:
            grid_row = first_row - margin + jnp.arange(widened.shape[0], dtype=jnp.int32)
            inside = (grid_row >= 0) & (grid_row < bands * tile_rows)
            widened = jnp.where(inside[:, None, None], widened, jnp.zeros_like(widened))
    return widened


def solution(mesh):
    in_specs = (
        P(("lat", "lon"), None, None, None),
        P(),
        P(),
        P(("lat", "lon"), None),
        P(("lat", "lon")),
        P(("lat", "lon")),
        P(("lat", "lon"), None, None),
        P(("lat", "lon"), None, None),
        P("lat", "lon", None),
        P(),
        P(),
        P(),
        P(),
    )
    out_specs = P("lat", "lon", None)
    return jax.shard_map(
        per_device, mesh=mesh, in_specs=in_specs, out_specs=out_specs, check_vma=False
    )
```

```python
import jax
import jax.numpy as jnp
from jax import lax
from jax.sharding import PartitionSpec as P

KS = 7
HALO = 3
LAYERS = 2
CAP = 2
RB = 16
RW = 16


def shifted(value, axis, steps):
    count = lax.axis_size(axis)
    leading, last = (max(0, -steps), min(count, count - steps))
    return lax.ppermute(value, axis, [(source, source + steps) for source in range(leading, last)])


def resample_local(blocks, row_mix, col_mix):
    row_mixed = jnp.einsum("nri,nijc->nrjc", row_mix, blocks, preferred_element_type=jnp.float32)
    both_mixed = jnp.einsum(
        "nrjc,nuj->nruc", row_mixed, col_mix.astype(jnp.float32), precision=lax.Precision.HIGHEST
    )
    return both_mixed.astype(jnp.bfloat16)


def place_rows(onehot, values):
    flat_values = values.reshape(values.shape[0], -1)
    placed = jnp.dot(onehot.astype(values.dtype), flat_values, preferred_element_type=jnp.float32)
    return placed.astype(values.dtype).reshape((onehot.shape[0],) + values.shape[1:])


def place_ints(onehot, values):
    return jnp.sum(jnp.where(onehot, values[None, :], 0), axis=1)


def keep_local(keep, values):
    shaped = keep.reshape((keep.shape[0],) + (1,) * (values.ndim - 1))
    return jnp.where(shaped, values, jnp.zeros_like(values))


def depthwise(widened, depth_kernel, height, width):
    mixed = None
    for e in range(KS):
        column = widened[:, e : e + width]
        for a in range(KS):
            term = column[a : a + height] * depth_kernel[a, e]
            mixed = term if mixed is None else mixed + term
    return mixed


def layer_apply(padded, depth_kernel, gain, up_matrix, down_matrix):
    height = padded.shape[0] - (KS - 1)
    width = padded.shape[1] - (KS - 1)
    spare = -width % 8
    widened = padded.astype(jnp.float32)
    if spare:
        widened = jnp.pad(widened, ((0, 0), (0, spare), (0, 0)))
    mixed = depthwise(widened, depth_kernel, height, width + spare)
    centered = mixed - jnp.mean(mixed, axis=-1, keepdims=True)
    variance = jnp.mean(centered * centered, axis=-1, keepdims=True)
    normed = (centered * lax.rsqrt(variance + 1e-06) * gain).astype(jnp.bfloat16)
    flat_cells = normed.reshape(height * (width + spare), -1)
    hidden = jax.nn.gelu(jnp.dot(flat_cells, up_matrix, preferred_element_type=jnp.float32)).astype(
        jnp.bfloat16
    )
    output = jnp.dot(hidden, down_matrix, preferred_element_type=jnp.float32).reshape(
        height, width + spare, -1
    )
    residual_part = widened[HALO : HALO + height, HALO : HALO + width + spare]
    return (residual_part + output).astype(jnp.bfloat16)[:, :width]


def per_device(
    swath_input,
    conv_weight,
    conv_bias,
    block_band,
    row_offset,
    col_offset,
    row_weights,
    col_weights,
    background,
    depth_weight,
    norm_gain,
    up_weight,
    down_weight,
):
    blocks_here = swath_input.shape[0]
    tile_rows = background.shape[0]
    tile_cols = background.shape[1]
    channels = background.shape[2]
    bands = lax.axis_size("lat")
    convolved = lax.conv_general_dilated(
        swath_input,
        conv_weight,
        (2, 2),
        ((1, 1), (1, 1)),
        dimension_numbers=("NHWC", "HWIO", "NHWC"),
        preferred_element_type=jnp.float32,
    )
    features = jax.nn.gelu(convolved + conv_bias).astype(jnp.bfloat16)
    resampled = resample_local(features, row_weights, col_weights)
    own_band = lax.axis_index("lat")
    reach = HALO * LAYERS
    lane = jnp.arange(channels, dtype=jnp.int32)[None, :]

    def with_header(blocks, rows, cols, bands_of):
        header = jnp.where(
            lane == 0,
            rows[:, None],
            jnp.where(lane == 1, cols[:, None], jnp.where(lane == 2, bands_of[:, None], 0)),
        ).astype(jnp.bfloat16)
        header = jnp.broadcast_to(header[:, None, None, :], (blocks.shape[0], 1, RW, channels))
        return jnp.concatenate([blocks, header], axis=1)

    def split_header(got):
        got_header = got[:, RB, 0, :].astype(jnp.int32)
        return got[:, :RB], got_header[:, 0], got_header[:, 1], got_header[:, 2]

    own_bands = block_band[:, 0]
    mine = with_header(resampled, row_offset, col_offset, own_bands)
    block_list, row_list, col_list, band_list = [resampled], [row_offset], [col_offset], [own_bands]
    positions = jnp.arange(blocks_here, dtype=jnp.int32)
    for step in (1, -1):
        edge = background[-reach:] if step == 1 else background[:reach]
        near_payload = jnp.concatenate(
            [mine.reshape(-1, channels), edge.reshape(-1, channels)], axis=0
        )
        going = own_bands - own_band == step
        earlier = jnp.sum(going[None, :] & (positions[None, :] < positions[:, None]), axis=1)
        table = (jnp.arange(CAP, dtype=jnp.int32)[:, None] == earlier[None, :]) & going[None, :]
        far_payload = with_header(
            place_rows(table, resampled),
            place_ints(table, row_offset),
            place_ints(table, col_offset),
            place_ints(table, own_bands),
        )
        got_near = shifted(near_payload, "lat", step)
        got_far = shifted(far_payload, "lat", 2 * step)
        near_blocks = got_near[: mine.shape[0] * mine.shape[1] * RW].reshape(mine.shape)
        got_edge = got_near[mine.shape[0] * mine.shape[1] * RW :].reshape(edge.shape)
        for got in (near_blocks, got_far):
            blocks, rows, cols, bands_of = split_header(got)
            block_list.append(blocks)
            row_list.append(rows)
            col_list.append(cols)
            band_list.append(bands_of)
        if step == 1:
            north_edge = got_edge
        else:
            south_edge = got_edge
    arrived = jnp.concatenate(block_list, axis=0)
    all_rows = (jnp.concatenate(band_list, axis=0) - own_band) * tile_rows + jnp.concatenate(
        row_list, axis=0
    ) + reach
    all_cols = jnp.concatenate(col_list, axis=0)
    ext_rows = tile_rows + 2 * reach
    row_place = (
        jnp.arange(ext_rows, dtype=jnp.int32)[None, :, None]
        == all_rows[:, None, None] + jnp.arange(RB, dtype=jnp.int32)[None, None, :]
    ).astype(jnp.bfloat16)
    col_place = (
        jnp.arange(tile_cols, dtype=jnp.int32)[None, :, None]
        == all_cols[:, None, None] + jnp.arange(RW, dtype=jnp.int32)[None, None, :]
    ).astype(jnp.bfloat16)
    lifted = jnp.einsum(
        "shr,sruc->shuc", row_place, arrived, preferred_element_type=jnp.float32
    ).astype(jnp.bfloat16)
    summed = jnp.einsum("swu,shuc->hwc", col_place, lifted, preferred_element_type=jnp.float32)
    ground = jnp.concatenate([north_edge, background, south_edge], axis=0)
    state = (ground.astype(jnp.float32) + summed).astype(jnp.bfloat16)
    tiles = lax.axis_size("lon")
    west = lax.ppermute(state[:, -reach:], "lon", [(i, (i + 1) % tiles) for i in range(tiles)])
    east = lax.ppermute(state[:, :reach], "lon", [((i + 1) % tiles, i) for i in range(tiles)])
    widened = jnp.concatenate([west, state, east], axis=1)
    first_row = own_band * tile_rows
    for layer_index in range(LAYERS):
        widened = layer_apply(
            widened,
            depth_weight[layer_index],
            norm_gain[layer_index],
            up_weight[layer_index],
            down_weight[layer_index],
        )
        margin = (widened.shape[0] - tile_rows) // 2
        if margin:
            grid_row = first_row - margin + jnp.arange(widened.shape[0], dtype=jnp.int32)
            inside = (grid_row >= 0) & (grid_row < bands * tile_rows)
            widened = jnp.where(inside[:, None, None], widened, jnp.zeros_like(widened))
    return widened


def solution(mesh):
    in_specs = (
        P(("lat", "lon"), None, None, None),
        P(),
        P(),
        P(("lat", "lon"), None),
        P(("lat", "lon")),
        P(("lat", "lon")),
        P(("lat", "lon"), None, None),
        P(("lat", "lon"), None, None),
        P("lat", "lon", None),
        P(),
        P(),
        P(),
        P(),
    )
    out_specs = P("lat", "lon", None)
    return jax.shard_map(
        per_device, mesh=mesh, in_specs=in_specs, out_specs=out_specs, check_vma=False
    )
```

```python
import jax
import jax.numpy as jnp
from jax import lax
from jax.sharding import PartitionSpec as P

KS = 7
HALO = 3
LAYERS = 2
CAP = 2
RB = 16
RW = 16


def shifted(value, axis, steps):
    count = lax.axis_size(axis)
    leading, last = (max(0, -steps), min(count, count - steps))
    return lax.ppermute(value, axis, [(source, source + steps) for source in range(leading, last)])


def with_halo(value, sides, width, wrap):
    for axis, dim in sides:
        size, length = (lax.axis_size(axis), value.shape[dim])
        up = [(i, (i + 1) % size) for i in range(size if wrap else size - 1)]
        down = [(j, i) for i, j in up]
        last = lax.slice_in_dim(value, length - width, length, axis=dim)
        leading = lax.slice_in_dim(value, 0, width, axis=dim)
        before = lax.ppermute(last, axis, up)
        after = lax.ppermute(leading, axis, down)
        value = jnp.concatenate([before, value, after], axis=dim)
    return value


def resample_local(blocks, row_mix, col_mix):
    row_mixed = jnp.einsum("nri,nijc->nrjc", row_mix, blocks, preferred_element_type=jnp.float32)
    both_mixed = jnp.einsum(
        "nrjc,nuj->nruc", row_mixed, col_mix.astype(jnp.float32), precision=lax.Precision.HIGHEST
    )
    return both_mixed.astype(jnp.bfloat16)


def place_rows(onehot, values):
    flat_values = values.reshape(values.shape[0], -1)
    placed = jnp.dot(onehot.astype(values.dtype), flat_values, preferred_element_type=jnp.float32)
    return placed.astype(values.dtype).reshape((onehot.shape[0],) + values.shape[1:])


def place_ints(onehot, values):
    return jnp.sum(jnp.where(onehot, values[None, :], 0), axis=1)


def keep_local(keep, values):
    shaped = keep.reshape((keep.shape[0],) + (1,) * (values.ndim - 1))
    return jnp.where(shaped, values, jnp.zeros_like(values))


def depthwise(widened, depth_kernel, height, width):
    mixed = None
    for e in range(KS):
        column = widened[:, e : e + width]
        for a in range(KS):
            term = column[a : a + height] * depth_kernel[a, e]
            mixed = term if mixed is None else mixed + term
    return mixed


def layer_apply(padded, depth_kernel, gain, up_matrix, down_matrix):
    height = padded.shape[0] - (KS - 1)
    width = padded.shape[1] - (KS - 1)
    spare = -width % 8
    widened = padded.astype(jnp.float32)
    if spare:
        widened = jnp.pad(widened, ((0, 0), (0, spare), (0, 0)))
    mixed = depthwise(widened, depth_kernel, height, width + spare)
    centered = mixed - jnp.mean(mixed, axis=-1, keepdims=True)
    variance = jnp.mean(centered * centered, axis=-1, keepdims=True)
    normed = (centered * lax.rsqrt(variance + 1e-06) * gain).astype(jnp.bfloat16)
    flat_cells = normed.reshape(height * (width + spare), -1)
    hidden = jax.nn.gelu(jnp.dot(flat_cells, up_matrix, preferred_element_type=jnp.float32)).astype(
        jnp.bfloat16
    )
    output = jnp.dot(hidden, down_matrix, preferred_element_type=jnp.float32).reshape(
        height, width + spare, -1
    )
    residual_part = widened[HALO : HALO + height, HALO : HALO + width + spare]
    return (residual_part + output).astype(jnp.bfloat16)[:, :width]


def per_device(
    swath_input,
    conv_weight,
    conv_bias,
    block_band,
    row_offset,
    col_offset,
    row_weights,
    col_weights,
    background,
    depth_weight,
    norm_gain,
    up_weight,
    down_weight,
):
    blocks_here = swath_input.shape[0]
    tile_rows = background.shape[0]
    tile_cols = background.shape[1]
    channels = background.shape[2]
    bands = lax.axis_size("lat")
    convolved = lax.conv_general_dilated(
        swath_input,
        conv_weight,
        (2, 2),
        ((1, 1), (1, 1)),
        dimension_numbers=("NHWC", "HWIO", "NHWC"),
        preferred_element_type=jnp.float32,
    )
    features = jax.nn.gelu(convolved + conv_bias).astype(jnp.bfloat16)
    resampled = resample_local(features, row_weights, col_weights)
    own_band = lax.axis_index("lat")
    offset_band = block_band[:, 0] - own_band
    staying = offset_band == 0
    positions = jnp.arange(blocks_here, dtype=jnp.int32)
    row_list = [row_offset]
    col_list = [col_offset]
    block_list = [keep_local(staying, resampled)]
    for step in (1, -1):
        going = offset_band == step
        earlier = jnp.sum(going[None, :] & (positions[None, :] < positions[:, None]), axis=1)
        table = (jnp.arange(CAP, dtype=jnp.int32)[:, None] == earlier[None, :]) & going[None, :]
        sent_blocks = place_rows(table, resampled)
        sent_rows = place_ints(table, row_offset)
        sent_cols = place_ints(table, col_offset)
        lane = jnp.arange(channels, dtype=jnp.int32)[None, :]
        header = jnp.where(
            lane == 0, sent_rows[:, None], jnp.where(lane == 1, sent_cols[:, None], 0)
        ).astype(jnp.bfloat16)
        header = jnp.broadcast_to(header[:, None, None, :], (CAP, 1, RW, channels))
        payload = jnp.concatenate([sent_blocks, header], axis=1)
        got = shifted(payload, "lat", step)
        block_list.append(got[:, :RB])
        got_header = got[:, RB, 0, :].astype(jnp.int32)
        row_list.append(got_header[:, 0])
        col_list.append(got_header[:, 1])
    arrived = jnp.concatenate(block_list, axis=0)
    all_rows = jnp.concatenate(row_list, axis=0)
    all_cols = jnp.concatenate(col_list, axis=0)
    row_place = (
        jnp.arange(tile_rows, dtype=jnp.int32)[None, :, None]
        == all_rows[:, None, None] + jnp.arange(RB, dtype=jnp.int32)[None, None, :]
    ).astype(jnp.bfloat16)
    col_place = (
        jnp.arange(tile_cols, dtype=jnp.int32)[None, :, None]
        == all_cols[:, None, None] + jnp.arange(RW, dtype=jnp.int32)[None, None, :]
    ).astype(jnp.bfloat16)
    lifted = jnp.einsum(
        "shr,sruc->shuc", row_place, arrived, preferred_element_type=jnp.float32
    ).astype(jnp.bfloat16)
    summed = jnp.einsum("swu,shuc->hwc", col_place, lifted, preferred_element_type=jnp.float32)
    state = (background.astype(jnp.float32) + summed).astype(jnp.bfloat16)
    reach = HALO * LAYERS
    widened = with_halo(state, (("lon", 1),), reach, True)
    widened = with_halo(widened, (("lat", 0),), reach, False)
    first_row = own_band * tile_rows
    for layer_index in range(LAYERS):
        widened = layer_apply(
            widened,
            depth_weight[layer_index],
            norm_gain[layer_index],
            up_weight[layer_index],
            down_weight[layer_index],
        )
        margin = (widened.shape[0] - tile_rows) // 2
        if margin:
            grid_row = first_row - margin + jnp.arange(widened.shape[0], dtype=jnp.int32)
            inside = (grid_row >= 0) & (grid_row < bands * tile_rows)
            widened = jnp.where(inside[:, None, None], widened, jnp.zeros_like(widened))
    return widened


def solution(mesh):
    in_specs = (
        P(("lat", "lon"), None, None, None),
        P(),
        P(),
        P(("lat", "lon"), None),
        P(("lat", "lon")),
        P(("lat", "lon")),
        P(("lat", "lon"), None, None),
        P(("lat", "lon"), None, None),
        P("lat", "lon", None),
        P(),
        P(),
        P(),
        P(),
    )
    out_specs = P("lat", "lon", None)
    return jax.shard_map(
        per_device, mesh=mesh, in_specs=in_specs, out_specs=out_specs, check_vma=False
    )
```

```python
import jax
import jax.numpy as jnp
from jax import lax
from jax.experimental import pallas as pl
from jax.experimental.pallas import tpu as pltpu
from jax.sharding import PartitionSpec as P

KS = 7
HALO = 3
LAYERS = 2
CAP = 2
RB = 16
RW = 16


def _conv_body(x_ref, w_ref, b_ref, o_ref, wide_ref):
    oh, ow, ch = o_ref.shape[1], o_ref.shape[2], o_ref.shape[3]
    cin = x_ref.shape[3]
    lanes = wide_ref.shape[3]
    parts = wide_ref.shape[0]
    for part in range(parts):
        wide_ref[part] = x_ref[0, :, :, part * lanes : (part + 1) * lanes].astype(jnp.float32)

    def parity(rp, cp):
        halves = [
            wide_ref[part, pl.ds(rp, oh, stride=2), pl.ds(cp, ow, stride=2), :].astype(x_ref.dtype)
            for part in range(parts)
        ]
        v = jnp.concatenate(halves, axis=-1)
        return v.reshape(oh * ow, cin)

    def tap(v, a, e):
        return jnp.dot(v, w_ref[a, e], preferred_element_type=jnp.float32)

    even_even, even_odd = parity(0, 0), parity(0, 1)
    odd_even, odd_odd = parity(1, 0), parity(1, 1)
    plain = tap(even_even, 1, 1) + tap(even_odd, 1, 2) + tap(odd_even, 2, 1) + tap(odd_odd, 2, 2)
    row_shift = tap(odd_even, 0, 1) + tap(odd_odd, 0, 2)
    col_shift = tap(even_odd, 1, 0) + tap(odd_odd, 2, 0)
    both_shift = tap(odd_odd, 0, 0)
    plain = plain.reshape(oh, ow, ch)
    row_shift = row_shift.reshape(oh, ow, ch)
    col_shift = col_shift.reshape(oh, ow, ch)
    both_shift = both_shift.reshape(oh, ow, ch)
    zero_row = jnp.zeros((1, ow, ch), jnp.float32)
    col_part = col_shift + jnp.concatenate([zero_row, both_shift[:-1]], axis=0)
    total = plain + jnp.concatenate([zero_row, row_shift[:-1]], axis=0)
    rolled = pltpu.roll(col_part, 1, 1)
    first_col = lax.broadcasted_iota(jnp.int32, (oh, ow, ch), 1) == 0
    total = total + jnp.where(first_col, 0.0, rolled)
    total = total + b_ref[...]
    o_ref[0] = jax.nn.gelu(total).astype(o_ref.dtype)


def conv_gelu(x, w, b):
    n, h, wd, cin = x.shape
    cout = w.shape[3]
    oh, ow = h // 2, wd // 2
    return pl.pallas_call(
        _conv_body,
        grid=(n,),
        in_specs=[
            pl.BlockSpec((1, h, wd, cin), lambda i: (i, 0, 0, 0)),
            pl.BlockSpec((3, 3, cin, cout), lambda i: (0, 0, 0, 0)),
            pl.BlockSpec((1, cout), lambda i: (0, 0)),
        ],
        out_specs=pl.BlockSpec((1, oh, ow, cout), lambda i: (i, 0, 0, 0)),
        out_shape=jax.ShapeDtypeStruct((n, oh, ow, cout), jnp.bfloat16),
        scratch_shapes=[pltpu.VMEM((cin // 128, h, wd, 128), jnp.float32)],
        compiler_params=pltpu.CompilerParams(dimension_semantics=("arbitrary",)),
    )(x, w, b.reshape(1, cout))


def shifted(value, axis, steps):
    count = lax.axis_size(axis)
    leading, last = (max(0, -steps), min(count, count - steps))
    return lax.ppermute(value, axis, [(source, source + steps) for source in range(leading, last)])


def with_halo(value, sides, width, wrap):
    for axis, dim in sides:
        size, length = (lax.axis_size(axis), value.shape[dim])
        up = [(i, (i + 1) % size) for i in range(size if wrap else size - 1)]
        down = [(j, i) for i, j in up]
        last = lax.slice_in_dim(value, length - width, length, axis=dim)
        leading = lax.slice_in_dim(value, 0, width, axis=dim)
        before = lax.ppermute(last, axis, up)
        after = lax.ppermute(leading, axis, down)
        value = jnp.concatenate([before, value, after], axis=dim)
    return value


def resample_local(blocks, row_mix, col_mix):
    row_mixed = jnp.einsum("nri,nijc->nrjc", row_mix, blocks, preferred_element_type=jnp.float32)
    both_mixed = jnp.einsum(
        "nrjc,nuj->nruc", row_mixed, col_mix.astype(jnp.float32), precision=lax.Precision.HIGHEST
    )
    return both_mixed.astype(jnp.bfloat16)


def place_rows(onehot, values):
    flat_values = values.reshape(values.shape[0], -1)
    placed = jnp.dot(onehot.astype(values.dtype), flat_values, preferred_element_type=jnp.float32)
    return placed.astype(values.dtype).reshape((onehot.shape[0],) + values.shape[1:])


def place_ints(onehot, values):
    return jnp.sum(jnp.where(onehot, values[None, :], 0), axis=1)


def keep_local(keep, values):
    shaped = keep.reshape((keep.shape[0],) + (1,) * (values.ndim - 1))
    return jnp.where(shaped, values, jnp.zeros_like(values))


def depthwise(widened, depth_kernel, height, width):
    mixed = None
    for e in range(KS):
        column = widened[:, e : e + width]
        for a in range(KS):
            term = column[a : a + height] * depth_kernel[a, e]
            mixed = term if mixed is None else mixed + term
    return mixed


def layer_apply(padded, depth_kernel, gain, up_matrix, down_matrix):
    height = padded.shape[0] - (KS - 1)
    width = padded.shape[1] - (KS - 1)
    spare = -width % 8
    widened = padded.astype(jnp.float32)
    if spare:
        widened = jnp.pad(widened, ((0, 0), (0, spare), (0, 0)))
    mixed = depthwise(widened, depth_kernel, height, width + spare)
    centered = mixed - jnp.mean(mixed, axis=-1, keepdims=True)
    variance = jnp.mean(centered * centered, axis=-1, keepdims=True)
    normed = (centered * lax.rsqrt(variance + 1e-06) * gain).astype(jnp.bfloat16)
    flat_cells = normed.reshape(height * (width + spare), -1)
    hidden = jax.nn.gelu(jnp.dot(flat_cells, up_matrix, preferred_element_type=jnp.float32)).astype(
        jnp.bfloat16
    )
    output = jnp.dot(hidden, down_matrix, preferred_element_type=jnp.float32).reshape(
        height, width + spare, -1
    )
    residual_part = widened[HALO : HALO + height, HALO : HALO + width + spare]
    return (residual_part + output).astype(jnp.bfloat16)[:, :width]


def per_device(
    swath_input,
    conv_weight,
    conv_bias,
    block_band,
    row_offset,
    col_offset,
    row_weights,
    col_weights,
    background,
    depth_weight,
    norm_gain,
    up_weight,
    down_weight,
):
    blocks_here = swath_input.shape[0]
    tile_rows = background.shape[0]
    tile_cols = background.shape[1]
    channels = background.shape[2]
    bands = lax.axis_size("lat")
    features = conv_gelu(swath_input, conv_weight, conv_bias)
    resampled = resample_local(features, row_weights, col_weights)
    own_band = lax.axis_index("lat")
    offset_band = block_band[:, 0] - own_band
    staying = offset_band == 0
    positions = jnp.arange(blocks_here, dtype=jnp.int32)
    row_list = [row_offset]
    col_list = [col_offset]
    block_list = [keep_local(staying, resampled)]
    for step in (1, -1):
        going = offset_band == step
        earlier = jnp.sum(going[None, :] & (positions[None, :] < positions[:, None]), axis=1)
        table = (jnp.arange(CAP, dtype=jnp.int32)[:, None] == earlier[None, :]) & going[None, :]
        sent_blocks = place_rows(table, resampled)
        sent_rows = place_ints(table, row_offset)
        sent_cols = place_ints(table, col_offset)
        lane = jnp.arange(channels, dtype=jnp.int32)[None, :]
        header = jnp.where(
            lane == 0, sent_rows[:, None], jnp.where(lane == 1, sent_cols[:, None], 0)
        ).astype(jnp.bfloat16)
        header = jnp.broadcast_to(header[:, None, None, :], (CAP, 1, RW, channels))
        payload = jnp.concatenate([sent_blocks, header], axis=1)
        got = shifted(payload, "lat", step)
        block_list.append(got[:, :RB])
        got_header = got[:, RB, 0, :].astype(jnp.int32)
        row_list.append(got_header[:, 0])
        col_list.append(got_header[:, 1])
    arrived = jnp.concatenate(block_list, axis=0)
    all_rows = jnp.concatenate(row_list, axis=0)
    all_cols = jnp.concatenate(col_list, axis=0)
    row_place = (
        jnp.arange(tile_rows, dtype=jnp.int32)[None, :, None]
        == all_rows[:, None, None] + jnp.arange(RB, dtype=jnp.int32)[None, None, :]
    ).astype(jnp.bfloat16)
    col_place = (
        jnp.arange(tile_cols, dtype=jnp.int32)[None, :, None]
        == all_cols[:, None, None] + jnp.arange(RW, dtype=jnp.int32)[None, None, :]
    ).astype(jnp.bfloat16)
    lifted = jnp.einsum(
        "shr,sruc->shuc", row_place, arrived, preferred_element_type=jnp.float32
    ).astype(jnp.bfloat16)
    summed = jnp.einsum("swu,shuc->hwc", col_place, lifted, preferred_element_type=jnp.float32)
    state = (background.astype(jnp.float32) + summed).astype(jnp.bfloat16)
    reach = HALO * LAYERS
    widened = with_halo(state, (("lon", 1),), reach, True)
    widened = with_halo(widened, (("lat", 0),), reach, False)
    first_row = own_band * tile_rows
    for layer_index in range(LAYERS):
        widened = layer_apply(
            widened,
            depth_weight[layer_index],
            norm_gain[layer_index],
            up_weight[layer_index],
            down_weight[layer_index],
        )
        margin = (widened.shape[0] - tile_rows) // 2
        if margin:
            grid_row = first_row - margin + jnp.arange(widened.shape[0], dtype=jnp.int32)
            inside = (grid_row >= 0) & (grid_row < bands * tile_rows)
            widened = jnp.where(inside[:, None, None], widened, jnp.zeros_like(widened))
    return widened


def solution(mesh):
    in_specs = (
        P(("lat", "lon"), None, None, None),
        P(),
        P(),
        P(("lat", "lon"), None),
        P(("lat", "lon")),
        P(("lat", "lon")),
        P(("lat", "lon"), None, None),
        P(("lat", "lon"), None, None),
        P("lat", "lon", None),
        P(),
        P(),
        P(),
        P(),
    )
    out_specs = P("lat", "lon", None)
    return jax.shard_map(
        per_device, mesh=mesh, in_specs=in_specs, out_specs=out_specs, check_vma=False
    )
```

```python
import jax
import jax.numpy as jnp
from jax import lax
from jax.experimental import pallas as pl
from jax.experimental.pallas import tpu as pltpu
from jax.sharding import PartitionSpec as P

KS = 7
HALO = 3
LAYERS = 2
CAP = 2
RB = 16
RW = 16


def _conv_body(x_ref, w_ref, b_ref, high_ref, low_ref, o_ref, wide_ref):
    oh, ow, ch = x_ref.shape[1] // 2, x_ref.shape[2] // 2, o_ref.shape[2]
    cin = x_ref.shape[3]
    lanes = wide_ref.shape[3]
    parts = wide_ref.shape[0]
    for part in range(parts):
        wide_ref[part] = x_ref[0, :, :, part * lanes : (part + 1) * lanes].astype(jnp.float32)

    def parity(rp, cp):
        halves = [
            wide_ref[part, pl.ds(rp, oh, stride=2), pl.ds(cp, ow, stride=2), :].astype(x_ref.dtype)
            for part in range(parts)
        ]
        v = jnp.concatenate(halves, axis=-1)
        return v.reshape(oh * ow, cin)

    def tap(v, a, e):
        return jnp.dot(v, w_ref[a, e], preferred_element_type=jnp.float32)

    even_even, even_odd = parity(0, 0), parity(0, 1)
    odd_even, odd_odd = parity(1, 0), parity(1, 1)
    plain = tap(even_even, 1, 1) + tap(even_odd, 1, 2) + tap(odd_even, 2, 1) + tap(odd_odd, 2, 2)
    row_shift = tap(odd_even, 0, 1) + tap(odd_odd, 0, 2)
    col_shift = tap(even_odd, 1, 0) + tap(odd_odd, 2, 0)
    both_shift = tap(odd_odd, 0, 0)
    plain = plain.reshape(oh, ow, ch)
    row_shift = row_shift.reshape(oh, ow, ch)
    col_shift = col_shift.reshape(oh, ow, ch)
    both_shift = both_shift.reshape(oh, ow, ch)
    zero_row = jnp.zeros((1, ow, ch), jnp.float32)
    col_part = col_shift + jnp.concatenate([zero_row, both_shift[:-1]], axis=0)
    total = plain + jnp.concatenate([zero_row, row_shift[:-1]], axis=0)
    rolled = pltpu.roll(col_part, 1, 1)
    first_col = lax.broadcasted_iota(jnp.int32, (oh, ow, ch), 1) == 0
    total = total + jnp.where(first_col, 0.0, rolled)
    total = total + b_ref[...]
    features = jax.nn.gelu(total).astype(x_ref.dtype).reshape(oh * ow, ch)
    mixed = jnp.dot(high_ref[0], features, preferred_element_type=jnp.float32) + jnp.dot(
        low_ref[0], features, preferred_element_type=jnp.float32
    )
    o_ref[0] = mixed.astype(o_ref.dtype)


def conv_resample(x, w, b, row_mix, col_mix):
    n, h, wd, cin = x.shape
    cout = w.shape[3]
    oh, ow = h // 2, wd // 2
    rb, rw = row_mix.shape[1], col_mix.shape[1]
    both = (
        row_mix.astype(jnp.float32)[:, :, None, :, None] * col_mix.astype(jnp.float32)[:, None, :, None, :]
    ).reshape(n, rb * rw, oh * ow)
    high = both.astype(x.dtype)
    low = (both - high.astype(jnp.float32)).astype(x.dtype)
    out = pl.pallas_call(
        _conv_body,
        grid=(n,),
        in_specs=[
            pl.BlockSpec((1, h, wd, cin), lambda i: (i, 0, 0, 0)),
            pl.BlockSpec((3, 3, cin, cout), lambda i: (0, 0, 0, 0)),
            pl.BlockSpec((1, cout), lambda i: (0, 0)),
            pl.BlockSpec((1, rb * rw, oh * ow), lambda i: (i, 0, 0)),
            pl.BlockSpec((1, rb * rw, oh * ow), lambda i: (i, 0, 0)),
        ],
        out_specs=pl.BlockSpec((1, rb * rw, cout), lambda i: (i, 0, 0)),
        out_shape=jax.ShapeDtypeStruct((n, rb * rw, cout), jnp.bfloat16),
        scratch_shapes=[pltpu.VMEM((cin // 128, h, wd, 128), jnp.float32)],
        compiler_params=pltpu.CompilerParams(dimension_semantics=("arbitrary",)),
    )(x, w, b.reshape(1, cout), high, low)
    return out.reshape(n, rb, rw, cout)


def shifted(value, axis, steps):
    count = lax.axis_size(axis)
    leading, last = (max(0, -steps), min(count, count - steps))
    return lax.ppermute(value, axis, [(source, source + steps) for source in range(leading, last)])


def with_halo(value, sides, width, wrap):
    for axis, dim in sides:
        size, length = (lax.axis_size(axis), value.shape[dim])
        up = [(i, (i + 1) % size) for i in range(size if wrap else size - 1)]
        down = [(j, i) for i, j in up]
        last = lax.slice_in_dim(value, length - width, length, axis=dim)
        leading = lax.slice_in_dim(value, 0, width, axis=dim)
        before = lax.ppermute(last, axis, up)
        after = lax.ppermute(leading, axis, down)
        value = jnp.concatenate([before, value, after], axis=dim)
    return value


def place_rows(onehot, values):
    flat_values = values.reshape(values.shape[0], -1)
    placed = jnp.dot(onehot.astype(values.dtype), flat_values, preferred_element_type=jnp.float32)
    return placed.astype(values.dtype).reshape((onehot.shape[0],) + values.shape[1:])


def place_ints(onehot, values):
    return jnp.sum(jnp.where(onehot, values[None, :], 0), axis=1)


def keep_local(keep, values):
    shaped = keep.reshape((keep.shape[0],) + (1,) * (values.ndim - 1))
    return jnp.where(shaped, values, jnp.zeros_like(values))


def depthwise(widened, depth_kernel, height, width):
    mixed = None
    for e in range(KS):
        column = widened[:, e : e + width]
        for a in range(KS):
            term = column[a : a + height] * depth_kernel[a, e]
            mixed = term if mixed is None else mixed + term
    return mixed


def layer_apply(padded, depth_kernel, gain, up_matrix, down_matrix):
    height = padded.shape[0] - (KS - 1)
    width = padded.shape[1] - (KS - 1)
    spare = -width % 8
    widened = padded.astype(jnp.float32)
    if spare:
        widened = jnp.pad(widened, ((0, 0), (0, spare), (0, 0)))
    mixed = depthwise(widened, depth_kernel, height, width + spare)
    centered = mixed - jnp.mean(mixed, axis=-1, keepdims=True)
    variance = jnp.mean(centered * centered, axis=-1, keepdims=True)
    normed = (centered * lax.rsqrt(variance + 1e-06) * gain).astype(jnp.bfloat16)
    flat_cells = normed.reshape(height * (width + spare), -1)
    hidden = jax.nn.gelu(jnp.dot(flat_cells, up_matrix, preferred_element_type=jnp.float32)).astype(
        jnp.bfloat16
    )
    output = jnp.dot(hidden, down_matrix, preferred_element_type=jnp.float32).reshape(
        height, width + spare, -1
    )
    residual_part = widened[HALO : HALO + height, HALO : HALO + width + spare]
    return (residual_part + output).astype(jnp.bfloat16)[:, :width]


def per_device(
    swath_input,
    conv_weight,
    conv_bias,
    block_band,
    row_offset,
    col_offset,
    row_weights,
    col_weights,
    background,
    depth_weight,
    norm_gain,
    up_weight,
    down_weight,
):
    blocks_here = swath_input.shape[0]
    tile_rows = background.shape[0]
    tile_cols = background.shape[1]
    channels = background.shape[2]
    bands = lax.axis_size("lat")
    resampled = conv_resample(swath_input, conv_weight, conv_bias, row_weights, col_weights)
    own_band = lax.axis_index("lat")
    offset_band = block_band[:, 0] - own_band
    staying = offset_band == 0
    positions = jnp.arange(blocks_here, dtype=jnp.int32)
    row_list = [row_offset]
    col_list = [col_offset]
    block_list = [keep_local(staying, resampled)]
    for step in (1, -1):
        going = offset_band == step
        earlier = jnp.sum(going[None, :] & (positions[None, :] < positions[:, None]), axis=1)
        table = (jnp.arange(CAP, dtype=jnp.int32)[:, None] == earlier[None, :]) & going[None, :]
        sent_blocks = place_rows(table, resampled)
        sent_rows = place_ints(table, row_offset)
        sent_cols = place_ints(table, col_offset)
        lane = jnp.arange(channels, dtype=jnp.int32)[None, :]
        header = jnp.where(
            lane == 0, sent_rows[:, None], jnp.where(lane == 1, sent_cols[:, None], 0)
        ).astype(jnp.bfloat16)
        header = jnp.broadcast_to(header[:, None, None, :], (CAP, 1, RW, channels))
        payload = jnp.concatenate([sent_blocks, header], axis=1)
        got = shifted(payload, "lat", step)
        block_list.append(got[:, :RB])
        got_header = got[:, RB, 0, :].astype(jnp.int32)
        row_list.append(got_header[:, 0])
        col_list.append(got_header[:, 1])
    arrived = jnp.concatenate(block_list, axis=0)
    all_rows = jnp.concatenate(row_list, axis=0)
    all_cols = jnp.concatenate(col_list, axis=0)
    row_place = (
        jnp.arange(tile_rows, dtype=jnp.int32)[None, :, None]
        == all_rows[:, None, None] + jnp.arange(RB, dtype=jnp.int32)[None, None, :]
    ).astype(jnp.bfloat16)
    col_place = (
        jnp.arange(tile_cols, dtype=jnp.int32)[None, :, None]
        == all_cols[:, None, None] + jnp.arange(RW, dtype=jnp.int32)[None, None, :]
    ).astype(jnp.bfloat16)
    lifted = jnp.einsum(
        "shr,sruc->shuc", row_place, arrived, preferred_element_type=jnp.float32
    ).astype(jnp.bfloat16)
    summed = jnp.einsum("swu,shuc->hwc", col_place, lifted, preferred_element_type=jnp.float32)
    state = (background.astype(jnp.float32) + summed).astype(jnp.bfloat16)
    reach = HALO * LAYERS
    widened = with_halo(state, (("lon", 1),), reach, True)
    widened = with_halo(widened, (("lat", 0),), reach, False)
    first_row = own_band * tile_rows
    for layer_index in range(LAYERS):
        widened = layer_apply(
            widened,
            depth_weight[layer_index],
            norm_gain[layer_index],
            up_weight[layer_index],
            down_weight[layer_index],
        )
        margin = (widened.shape[0] - tile_rows) // 2
        if margin:
            grid_row = first_row - margin + jnp.arange(widened.shape[0], dtype=jnp.int32)
            inside = (grid_row >= 0) & (grid_row < bands * tile_rows)
            widened = jnp.where(inside[:, None, None], widened, jnp.zeros_like(widened))
    return widened


def solution(mesh):
    in_specs = (
        P(("lat", "lon"), None, None, None),
        P(),
        P(),
        P(("lat", "lon"), None),
        P(("lat", "lon")),
        P(("lat", "lon")),
        P(("lat", "lon"), None, None),
        P(("lat", "lon"), None, None),
        P("lat", "lon", None),
        P(),
        P(),
        P(),
        P(),
    )
    out_specs = P("lat", "lon", None)
    return jax.shard_map(
        per_device, mesh=mesh, in_specs=in_specs, out_specs=out_specs, check_vma=False
    )
```

```python
import jax
import jax.numpy as jnp
from jax import lax
from jax.experimental import pallas as pl
from jax.experimental.pallas import tpu as pltpu
from jax.sharding import PartitionSpec as P

KS = 7
HALO = 3
LAYERS = 2
CAP = 2
RB = 16
RW = 16


def _conv_body(x_ref, w_ref, b_ref, o_ref, wide_ref):
    oh, ow, ch = o_ref.shape[1], o_ref.shape[2], o_ref.shape[3]
    cin = x_ref.shape[3]
    lanes = wide_ref.shape[3]
    parts = wide_ref.shape[0]
    for part in range(parts):
        wide_ref[part] = x_ref[0, :, :, part * lanes : (part + 1) * lanes].astype(jnp.float32)

    def parity(rp, cp):
        halves = [
            wide_ref[part, pl.ds(rp, oh, stride=2), pl.ds(cp, ow, stride=2), :].astype(x_ref.dtype)
            for part in range(parts)
        ]
        v = jnp.concatenate(halves, axis=-1)
        return v.reshape(oh * ow, cin)

    def tap(v, a, e):
        return jnp.dot(v, w_ref[a, e], preferred_element_type=jnp.float32)

    even_even, even_odd = parity(0, 0), parity(0, 1)
    odd_even, odd_odd = parity(1, 0), parity(1, 1)
    plain = tap(even_even, 1, 1) + tap(even_odd, 1, 2) + tap(odd_even, 2, 1) + tap(odd_odd, 2, 2)
    row_shift = tap(odd_even, 0, 1) + tap(odd_odd, 0, 2)
    col_shift = tap(even_odd, 1, 0) + tap(odd_odd, 2, 0)
    both_shift = tap(odd_odd, 0, 0)
    plain = plain.reshape(oh, ow, ch)
    row_shift = row_shift.reshape(oh, ow, ch)
    col_shift = col_shift.reshape(oh, ow, ch)
    both_shift = both_shift.reshape(oh, ow, ch)
    zero_row = jnp.zeros((1, ow, ch), jnp.float32)
    col_part = col_shift + jnp.concatenate([zero_row, both_shift[:-1]], axis=0)
    total = plain + jnp.concatenate([zero_row, row_shift[:-1]], axis=0)
    rolled = pltpu.roll(col_part, 1, 1)
    first_col = lax.broadcasted_iota(jnp.int32, (oh, ow, ch), 1) == 0
    total = total + jnp.where(first_col, 0.0, rolled)
    total = total + b_ref[...]
    o_ref[0] = jax.nn.gelu(total).astype(o_ref.dtype)


def conv_gelu(x, w, b):
    n, h, wd, cin = x.shape
    cout = w.shape[3]
    oh, ow = h // 2, wd // 2
    return pl.pallas_call(
        _conv_body,
        grid=(n,),
        in_specs=[
            pl.BlockSpec((1, h, wd, cin), lambda i: (i, 0, 0, 0)),
            pl.BlockSpec((3, 3, cin, cout), lambda i: (0, 0, 0, 0)),
            pl.BlockSpec((1, cout), lambda i: (0, 0)),
        ],
        out_specs=pl.BlockSpec((1, oh, ow, cout), lambda i: (i, 0, 0, 0)),
        out_shape=jax.ShapeDtypeStruct((n, oh, ow, cout), jnp.bfloat16),
        scratch_shapes=[pltpu.VMEM((cin // 128, h, wd, 128), jnp.float32)],
        compiler_params=pltpu.CompilerParams(dimension_semantics=("arbitrary",)),
    )(x, w, b.reshape(1, cout))


def shifted(value, axis, steps):
    count = lax.axis_size(axis)
    leading, last = (max(0, -steps), min(count, count - steps))
    return lax.ppermute(value, axis, [(source, source + steps) for source in range(leading, last)])


def with_halo(value, sides, width, wrap):
    for axis, dim in sides:
        size, length = (lax.axis_size(axis), value.shape[dim])
        up = [(i, (i + 1) % size) for i in range(size if wrap else size - 1)]
        down = [(j, i) for i, j in up]
        last = lax.slice_in_dim(value, length - width, length, axis=dim)
        leading = lax.slice_in_dim(value, 0, width, axis=dim)
        before = lax.ppermute(last, axis, up)
        after = lax.ppermute(leading, axis, down)
        value = jnp.concatenate([before, value, after], axis=dim)
    return value


def resample_local(blocks, row_mix, col_mix):
    row_mixed = jnp.einsum("nri,nijc->nrjc", row_mix, blocks, preferred_element_type=jnp.float32)
    both_mixed = jnp.einsum(
        "nrjc,nuj->nruc", row_mixed, col_mix.astype(jnp.float32), precision=lax.Precision.HIGHEST
    )
    return both_mixed.astype(jnp.bfloat16)


def place_rows(onehot, values):
    flat_values = values.reshape(values.shape[0], -1)
    placed = jnp.dot(onehot.astype(values.dtype), flat_values, preferred_element_type=jnp.float32)
    return placed.astype(values.dtype).reshape((onehot.shape[0],) + values.shape[1:])


def place_ints(onehot, values):
    return jnp.sum(jnp.where(onehot, values[None, :], 0), axis=1)


def keep_local(keep, values):
    shaped = keep.reshape((keep.shape[0],) + (1,) * (values.ndim - 1))
    return jnp.where(shaped, values, jnp.zeros_like(values))


def depthwise(widened, depth_kernel, height, width):
    mixed = None
    for e in range(KS):
        column = widened[:, e : e + width]
        for a in range(KS):
            term = column[a : a + height] * depth_kernel[a, e]
            mixed = term if mixed is None else mixed + term
    return mixed


def layer_apply(padded, depth_kernel, gain, up_matrix, down_matrix):
    height = padded.shape[0] - (KS - 1)
    width = padded.shape[1] - (KS - 1)
    spare = -width % 8
    widened = padded.astype(jnp.float32)
    if spare:
        widened = jnp.pad(widened, ((0, 0), (0, spare), (0, 0)))
    mixed = depthwise(widened, depth_kernel, height, width + spare)
    centered = mixed - jnp.mean(mixed, axis=-1, keepdims=True)
    variance = jnp.mean(centered * centered, axis=-1, keepdims=True)
    normed = (centered * lax.rsqrt(variance + 1e-06) * gain).astype(jnp.bfloat16)
    flat_cells = normed.reshape(height * (width + spare), -1)
    hidden = jax.nn.gelu(jnp.dot(flat_cells, up_matrix, preferred_element_type=jnp.float32)).astype(
        jnp.bfloat16
    )
    output = jnp.dot(hidden, down_matrix, preferred_element_type=jnp.float32).reshape(
        height, width + spare, -1
    )
    residual_part = widened[HALO : HALO + height, HALO : HALO + width + spare]
    return (residual_part + output).astype(jnp.bfloat16)[:, :width]


def per_device(
    swath_input,
    conv_weight,
    conv_bias,
    block_band,
    row_offset,
    col_offset,
    row_weights,
    col_weights,
    background,
    depth_weight,
    norm_gain,
    up_weight,
    down_weight,
):
    blocks_here = swath_input.shape[0]
    tile_rows = background.shape[0]
    tile_cols = background.shape[1]
    channels = background.shape[2]
    bands = lax.axis_size("lat")
    features = conv_gelu(swath_input, conv_weight, conv_bias)
    resampled = resample_local(features, row_weights, col_weights)
    own_band = lax.axis_index("lat")
    offset_band = block_band[:, 0] - own_band
    staying = offset_band == 0
    positions = jnp.arange(blocks_here, dtype=jnp.int32)
    row_list = [row_offset]
    col_list = [col_offset]
    block_list = [keep_local(staying, resampled)]
    for step in (1, -1):
        going = offset_band == step
        earlier = jnp.sum(going[None, :] & (positions[None, :] < positions[:, None]), axis=1)
        table = (jnp.arange(CAP, dtype=jnp.int32)[:, None] == earlier[None, :]) & going[None, :]
        sent_blocks = place_rows(table, resampled)
        sent_rows = place_ints(table, row_offset)
        sent_cols = place_ints(table, col_offset)
        lane = jnp.arange(channels, dtype=jnp.int32)[None, :]
        header = jnp.where(
            lane == 0, sent_rows[:, None], jnp.where(lane == 1, sent_cols[:, None], 0)
        ).astype(jnp.bfloat16)
        header = jnp.broadcast_to(header[:, None, None, :], (CAP, 1, RW, channels))
        payload = jnp.concatenate([sent_blocks, header], axis=1)
        got = shifted(payload, "lat", step)
        block_list.append(got[:, :RB])
        got_header = got[:, RB, 0, :].astype(jnp.int32)
        row_list.append(got_header[:, 0])
        col_list.append(got_header[:, 1])
    arrived = jnp.concatenate(block_list, axis=0)
    all_rows = jnp.concatenate(row_list, axis=0)
    all_cols = jnp.concatenate(col_list, axis=0)
    row_place = (
        jnp.arange(tile_rows, dtype=jnp.int32)[None, :, None]
        == all_rows[:, None, None] + jnp.arange(RB, dtype=jnp.int32)[None, None, :]
    ).astype(jnp.bfloat16)
    col_place = (
        jnp.arange(tile_cols, dtype=jnp.int32)[None, :, None]
        == all_cols[:, None, None] + jnp.arange(RW, dtype=jnp.int32)[None, None, :]
    ).astype(jnp.bfloat16)
    lifted = jnp.einsum(
        "shr,sruc->shuc", row_place, arrived, preferred_element_type=jnp.float32
    ).astype(jnp.bfloat16)
    summed = jnp.einsum("swu,shuc->hwc", col_place, lifted, preferred_element_type=jnp.float32)
    state = (background.astype(jnp.float32) + summed).astype(jnp.bfloat16)
    reach = HALO * LAYERS
    lon_wide = with_halo(state, (("lon", 1),), reach, True)
    size, length = lax.axis_size("lat"), lon_wide.shape[0]
    up = [(i, i + 1) for i in range(size - 1)]
    down = [(j, i) for i, j in up]
    north = lax.ppermute(lon_wide[length - reach :], "lat", up)
    south = lax.ppermute(lon_wide[:reach], "lat", down)
    first = (
        depth_weight[0],
        norm_gain[0],
        up_weight[0],
        down_weight[0],
    )
    middle = layer_apply(lon_wide, *first)
    top = layer_apply(jnp.concatenate([north, lon_wide[:reach]], axis=0), *first)
    bottom = layer_apply(jnp.concatenate([lon_wide[length - reach :], south], axis=0), *first)
    widened = jnp.concatenate([top, middle, bottom], axis=0)
    first_row = own_band * tile_rows
    margin = (widened.shape[0] - tile_rows) // 2
    grid_row = first_row - margin + jnp.arange(widened.shape[0], dtype=jnp.int32)
    inside = (grid_row >= 0) & (grid_row < bands * tile_rows)
    widened = jnp.where(inside[:, None, None], widened, jnp.zeros_like(widened))
    for layer_index in range(1, LAYERS):
        widened = layer_apply(
            widened,
            depth_weight[layer_index],
            norm_gain[layer_index],
            up_weight[layer_index],
            down_weight[layer_index],
        )
    return widened


def solution(mesh):
    in_specs = (
        P(("lat", "lon"), None, None, None),
        P(),
        P(),
        P(("lat", "lon"), None),
        P(("lat", "lon")),
        P(("lat", "lon")),
        P(("lat", "lon"), None, None),
        P(("lat", "lon"), None, None),
        P("lat", "lon", None),
        P(),
        P(),
        P(),
        P(),
    )
    out_specs = P("lat", "lon", None)
    return jax.shard_map(
        per_device, mesh=mesh, in_specs=in_specs, out_specs=out_specs, check_vma=False
    )
```

```python
import jax
import jax.numpy as jnp
from jax import lax
from jax.experimental import pallas as pl
from jax.experimental.pallas import tpu as pltpu
from jax.sharding import PartitionSpec as P

KS = 7
HALO = 3
LAYERS = 2
CAP = 2
RB = 16
RW = 16


def _expand(count, size, by_block):
    rows = lax.broadcasted_iota(jnp.int32, (count, size), 0)
    cols = lax.broadcasted_iota(jnp.int32, (count, size), 1)
    group = count // size if by_block else 1
    picked = rows // group if by_block else rows % size
    return (picked == cols).astype(jnp.bfloat16)


def _conv_body(x_ref, w_ref, b_ref, r_ref, c_ref, o_ref, wide_ref):
    oh, ow, ch = x_ref.shape[1] // 2, x_ref.shape[2] // 2, o_ref.shape[2]
    cin = x_ref.shape[3]
    lanes = wide_ref.shape[3]
    parts = wide_ref.shape[0]
    for part in range(parts):
        wide_ref[part] = x_ref[0, :, :, part * lanes : (part + 1) * lanes].astype(jnp.float32)

    def parity(rp, cp):
        halves = [
            wide_ref[part, pl.ds(rp, oh, stride=2), pl.ds(cp, ow, stride=2), :].astype(x_ref.dtype)
            for part in range(parts)
        ]
        v = jnp.concatenate(halves, axis=-1)
        return v.reshape(oh * ow, cin)

    def tap(v, a, e):
        return jnp.dot(v, w_ref[a, e], preferred_element_type=jnp.float32)

    even_even, even_odd = parity(0, 0), parity(0, 1)
    odd_even, odd_odd = parity(1, 0), parity(1, 1)
    plain = tap(even_even, 1, 1) + tap(even_odd, 1, 2) + tap(odd_even, 2, 1) + tap(odd_odd, 2, 2)
    row_shift = tap(odd_even, 0, 1) + tap(odd_odd, 0, 2)
    col_shift = tap(even_odd, 1, 0) + tap(odd_odd, 2, 0)
    both_shift = tap(odd_odd, 0, 0)
    plain = plain.reshape(oh, ow, ch)
    row_shift = row_shift.reshape(oh, ow, ch)
    col_shift = col_shift.reshape(oh, ow, ch)
    both_shift = both_shift.reshape(oh, ow, ch)
    zero_row = jnp.zeros((1, ow, ch), jnp.float32)
    col_part = col_shift + jnp.concatenate([zero_row, both_shift[:-1]], axis=0)
    total = plain + jnp.concatenate([zero_row, row_shift[:-1]], axis=0)
    rolled = pltpu.roll(col_part, 1, 1)
    first_col = lax.broadcasted_iota(jnp.int32, (oh, ow, ch), 1) == 0
    total = total + jnp.where(first_col, 0.0, rolled)
    total = total + b_ref[...]
    features = jax.nn.gelu(total).astype(x_ref.dtype).reshape(oh * ow, ch)
    row_mix, col_mix = r_ref[0], c_ref[0]
    rb, rw = row_mix.shape[0], col_mix.shape[0]
    cells = rb * rw
    by_row = jnp.dot(_expand(cells, rb, True), row_mix, preferred_element_type=jnp.float32)
    by_col = jnp.dot(_expand(cells, rw, False), col_mix, preferred_element_type=jnp.float32)
    spread_row = jnp.dot(
        by_row.astype(x_ref.dtype), _expand(oh * ow, oh, True).T, preferred_element_type=jnp.float32
    )
    spread_col = jnp.dot(
        by_col.astype(x_ref.dtype), _expand(oh * ow, ow, False).T, preferred_element_type=jnp.float32
    )
    both = spread_row * spread_col
    high = both.astype(x_ref.dtype)
    low = (both - high.astype(jnp.float32)).astype(x_ref.dtype)
    mixed = jnp.dot(high, features, preferred_element_type=jnp.float32) + jnp.dot(
        low, features, preferred_element_type=jnp.float32
    )
    o_ref[0] = mixed.astype(o_ref.dtype)


def conv_resample(x, w, b, row_mix, col_mix):
    n, h, wd, cin = x.shape
    cout = w.shape[3]
    oh, ow = h // 2, wd // 2
    rb, rw = row_mix.shape[1], col_mix.shape[1]
    out = pl.pallas_call(
        _conv_body,
        grid=(n,),
        in_specs=[
            pl.BlockSpec((1, h, wd, cin), lambda i: (i, 0, 0, 0)),
            pl.BlockSpec((3, 3, cin, cout), lambda i: (0, 0, 0, 0)),
            pl.BlockSpec((1, cout), lambda i: (0, 0)),
            pl.BlockSpec((1, rb, oh), lambda i: (i, 0, 0)),
            pl.BlockSpec((1, rw, ow), lambda i: (i, 0, 0)),
        ],
        out_specs=pl.BlockSpec((1, rb * rw, cout), lambda i: (i, 0, 0)),
        out_shape=jax.ShapeDtypeStruct((n, rb * rw, cout), jnp.bfloat16),
        scratch_shapes=[pltpu.VMEM((cin // 128, h, wd, 128), jnp.float32)],
        compiler_params=pltpu.CompilerParams(dimension_semantics=("arbitrary",)),
    )(x, w, b.reshape(1, cout), row_mix, col_mix)
    return out.reshape(n, rb, rw, cout)


def shifted(value, axis, steps):
    count = lax.axis_size(axis)
    leading, last = (max(0, -steps), min(count, count - steps))
    return lax.ppermute(value, axis, [(source, source + steps) for source in range(leading, last)])


def with_halo(value, sides, width, wrap):
    for axis, dim in sides:
        size, length = (lax.axis_size(axis), value.shape[dim])
        up = [(i, (i + 1) % size) for i in range(size if wrap else size - 1)]
        down = [(j, i) for i, j in up]
        last = lax.slice_in_dim(value, length - width, length, axis=dim)
        leading = lax.slice_in_dim(value, 0, width, axis=dim)
        before = lax.ppermute(last, axis, up)
        after = lax.ppermute(leading, axis, down)
        value = jnp.concatenate([before, value, after], axis=dim)
    return value


def place_rows(onehot, values):
    flat_values = values.reshape(values.shape[0], -1)
    placed = jnp.dot(onehot.astype(values.dtype), flat_values, preferred_element_type=jnp.float32)
    return placed.astype(values.dtype).reshape((onehot.shape[0],) + values.shape[1:])


def place_ints(onehot, values):
    return jnp.sum(jnp.where(onehot, values[None, :], 0), axis=1)


def keep_local(keep, values):
    shaped = keep.reshape((keep.shape[0],) + (1,) * (values.ndim - 1))
    return jnp.where(shaped, values, jnp.zeros_like(values))


def depthwise(widened, depth_kernel, height, width):
    mixed = None
    for e in range(KS):
        column = widened[:, e : e + width]
        for a in range(KS):
            term = column[a : a + height] * depth_kernel[a, e]
            mixed = term if mixed is None else mixed + term
    return mixed


def layer_apply(padded, depth_kernel, gain, up_matrix, down_matrix):
    height = padded.shape[0] - (KS - 1)
    width = padded.shape[1] - (KS - 1)
    spare = -width % 8
    widened = padded.astype(jnp.float32)
    if spare:
        widened = jnp.pad(widened, ((0, 0), (0, spare), (0, 0)))
    mixed = depthwise(widened, depth_kernel, height, width + spare)
    centered = mixed - jnp.mean(mixed, axis=-1, keepdims=True)
    variance = jnp.mean(centered * centered, axis=-1, keepdims=True)
    normed = (centered * lax.rsqrt(variance + 1e-06) * gain).astype(jnp.bfloat16)
    flat_cells = normed.reshape(height * (width + spare), -1)
    hidden = jax.nn.gelu(jnp.dot(flat_cells, up_matrix, preferred_element_type=jnp.float32)).astype(
        jnp.bfloat16
    )
    output = jnp.dot(hidden, down_matrix, preferred_element_type=jnp.float32).reshape(
        height, width + spare, -1
    )
    residual_part = widened[HALO : HALO + height, HALO : HALO + width + spare]
    return (residual_part + output).astype(jnp.bfloat16)[:, :width]


def per_device(
    swath_input,
    conv_weight,
    conv_bias,
    block_band,
    row_offset,
    col_offset,
    row_weights,
    col_weights,
    background,
    depth_weight,
    norm_gain,
    up_weight,
    down_weight,
):
    blocks_here = swath_input.shape[0]
    tile_rows = background.shape[0]
    tile_cols = background.shape[1]
    channels = background.shape[2]
    bands = lax.axis_size("lat")
    resampled = conv_resample(swath_input, conv_weight, conv_bias, row_weights, col_weights)
    own_band = lax.axis_index("lat")
    offset_band = block_band[:, 0] - own_band
    staying = offset_band == 0
    positions = jnp.arange(blocks_here, dtype=jnp.int32)
    row_list = [row_offset]
    col_list = [col_offset]
    block_list = [keep_local(staying, resampled)]
    for step in (1, -1):
        going = offset_band == step
        earlier = jnp.sum(going[None, :] & (positions[None, :] < positions[:, None]), axis=1)
        table = (jnp.arange(CAP, dtype=jnp.int32)[:, None] == earlier[None, :]) & going[None, :]
        sent_blocks = place_rows(table, resampled)
        sent_rows = place_ints(table, row_offset)
        sent_cols = place_ints(table, col_offset)
        lane = jnp.arange(channels, dtype=jnp.int32)[None, :]
        header = jnp.where(
            lane == 0, sent_rows[:, None], jnp.where(lane == 1, sent_cols[:, None], 0)
        ).astype(jnp.bfloat16)
        header = jnp.broadcast_to(header[:, None, None, :], (CAP, 1, RW, channels))
        payload = jnp.concatenate([sent_blocks, header], axis=1)
        got = shifted(payload, "lat", step)
        block_list.append(got[:, :RB])
        got_header = got[:, RB, 0, :].astype(jnp.int32)
        row_list.append(got_header[:, 0])
        col_list.append(got_header[:, 1])
    arrived = jnp.concatenate(block_list, axis=0)
    all_rows = jnp.concatenate(row_list, axis=0)
    all_cols = jnp.concatenate(col_list, axis=0)
    row_place = (
        jnp.arange(tile_rows, dtype=jnp.int32)[None, :, None]
        == all_rows[:, None, None] + jnp.arange(RB, dtype=jnp.int32)[None, None, :]
    ).astype(jnp.bfloat16)
    col_place = (
        jnp.arange(tile_cols, dtype=jnp.int32)[None, :, None]
        == all_cols[:, None, None] + jnp.arange(RW, dtype=jnp.int32)[None, None, :]
    ).astype(jnp.bfloat16)
    lifted = jnp.einsum(
        "shr,sruc->shuc", row_place, arrived, preferred_element_type=jnp.float32
    ).astype(jnp.bfloat16)
    summed = jnp.einsum("swu,shuc->hwc", col_place, lifted, preferred_element_type=jnp.float32)
    state = (background.astype(jnp.float32) + summed).astype(jnp.bfloat16)
    reach = HALO * LAYERS
    lon_wide = with_halo(state, (("lon", 1),), reach, True)
    size, length = lax.axis_size("lat"), lon_wide.shape[0]
    up = [(i, i + 1) for i in range(size - 1)]
    down = [(j, i) for i, j in up]
    north = lax.ppermute(lon_wide[length - reach :], "lat", up)
    south = lax.ppermute(lon_wide[:reach], "lat", down)
    first = (
        depth_weight[0],
        norm_gain[0],
        up_weight[0],
        down_weight[0],
    )
    middle = layer_apply(lon_wide, *first)
    top = layer_apply(jnp.concatenate([north, lon_wide[:reach]], axis=0), *first)
    bottom = layer_apply(jnp.concatenate([lon_wide[length - reach :], south], axis=0), *first)
    widened = jnp.concatenate([top, middle, bottom], axis=0)
    first_row = own_band * tile_rows
    margin = (widened.shape[0] - tile_rows) // 2
    grid_row = first_row - margin + jnp.arange(widened.shape[0], dtype=jnp.int32)
    inside = (grid_row >= 0) & (grid_row < bands * tile_rows)
    widened = jnp.where(inside[:, None, None], widened, jnp.zeros_like(widened))
    for layer_index in range(1, LAYERS):
        widened = layer_apply(
            widened,
            depth_weight[layer_index],
            norm_gain[layer_index],
            up_weight[layer_index],
            down_weight[layer_index],
        )
    return widened


def solution(mesh):
    in_specs = (
        P(("lat", "lon"), None, None, None),
        P(),
        P(),
        P(("lat", "lon"), None),
        P(("lat", "lon")),
        P(("lat", "lon")),
        P(("lat", "lon"), None, None),
        P(("lat", "lon"), None, None),
        P("lat", "lon", None),
        P(),
        P(),
        P(),
        P(),
    )
    out_specs = P("lat", "lon", None)
    return jax.shard_map(
        per_device, mesh=mesh, in_specs=in_specs, out_specs=out_specs, check_vma=False
    )
```

```python
import jax
import jax.numpy as jnp
from jax import lax
from jax.experimental import pallas as pl
from jax.experimental.pallas import tpu as pltpu
from jax.sharding import PartitionSpec as P

KS = 7
HALO = 3
LAYERS = 2
CAP = 2
RB = 16
RW = 16


def _expand(count, size, by_block):
    rows = lax.broadcasted_iota(jnp.int32, (count, size), 0)
    cols = lax.broadcasted_iota(jnp.int32, (count, size), 1)
    group = count // size if by_block else 1
    picked = rows // group if by_block else rows % size
    return (picked == cols).astype(jnp.bfloat16)


def _conv_body(x_ref, w_ref, b_ref, r_ref, c_ref, o_ref, wide_ref):
    oh, ow, ch = x_ref.shape[1] // 2, x_ref.shape[2] // 2, o_ref.shape[2]
    cin = x_ref.shape[3]
    lanes = wide_ref.shape[3]
    parts = wide_ref.shape[0]
    for part in range(parts):
        wide_ref[part] = x_ref[0, :, :, part * lanes : (part + 1) * lanes].astype(jnp.float32)

    def parity(rp, cp):
        halves = [
            wide_ref[part, pl.ds(rp, oh, stride=2), pl.ds(cp, ow, stride=2), :].astype(x_ref.dtype)
            for part in range(parts)
        ]
        v = jnp.concatenate(halves, axis=-1)
        return v.reshape(oh * ow, cin)

    def tap(v, a, e):
        return jnp.dot(v, w_ref[a, e], preferred_element_type=jnp.float32)

    even_even, even_odd = parity(0, 0), parity(0, 1)
    odd_even, odd_odd = parity(1, 0), parity(1, 1)
    plain = tap(even_even, 1, 1) + tap(even_odd, 1, 2) + tap(odd_even, 2, 1) + tap(odd_odd, 2, 2)
    row_shift = tap(odd_even, 0, 1) + tap(odd_odd, 0, 2)
    col_shift = tap(even_odd, 1, 0) + tap(odd_odd, 2, 0)
    both_shift = tap(odd_odd, 0, 0)
    plain = plain.reshape(oh, ow, ch)
    row_shift = row_shift.reshape(oh, ow, ch)
    col_shift = col_shift.reshape(oh, ow, ch)
    both_shift = both_shift.reshape(oh, ow, ch)
    zero_row = jnp.zeros((1, ow, ch), jnp.float32)
    col_part = col_shift + jnp.concatenate([zero_row, both_shift[:-1]], axis=0)
    total = plain + jnp.concatenate([zero_row, row_shift[:-1]], axis=0)
    rolled = pltpu.roll(col_part, 1, 1)
    first_col = lax.broadcasted_iota(jnp.int32, (oh, ow, ch), 1) == 0
    total = total + jnp.where(first_col, 0.0, rolled)
    total = total + b_ref[...]
    features = jax.nn.gelu(total).astype(x_ref.dtype).reshape(oh * ow, ch)
    row_mix, col_mix = r_ref[0], c_ref[0]
    rb, rw = row_mix.shape[0], col_mix.shape[0]
    cells = rb * rw
    by_row = jnp.dot(_expand(cells, rb, True), row_mix, preferred_element_type=jnp.float32)
    by_col = jnp.dot(_expand(cells, rw, False), col_mix, preferred_element_type=jnp.float32)
    spread_row = jnp.dot(
        by_row.astype(x_ref.dtype), _expand(oh * ow, oh, True).T, preferred_element_type=jnp.float32
    )
    spread_col = jnp.dot(
        by_col.astype(x_ref.dtype), _expand(oh * ow, ow, False).T, preferred_element_type=jnp.float32
    )
    both = spread_row * spread_col
    high = both.astype(x_ref.dtype)
    low = (both - high.astype(jnp.float32)).astype(x_ref.dtype)
    mixed = jnp.dot(high, features, preferred_element_type=jnp.float32) + jnp.dot(
        low, features, preferred_element_type=jnp.float32
    )
    o_ref[0] = mixed.astype(o_ref.dtype)


def conv_resample(x, w, b, row_mix, col_mix):
    n, h, wd, cin = x.shape
    cout = w.shape[3]
    oh, ow = h // 2, wd // 2
    rb, rw = row_mix.shape[1], col_mix.shape[1]
    out = pl.pallas_call(
        _conv_body,
        grid=(n,),
        in_specs=[
            pl.BlockSpec((1, h, wd, cin), lambda i: (i, 0, 0, 0)),
            pl.BlockSpec((3, 3, cin, cout), lambda i: (0, 0, 0, 0)),
            pl.BlockSpec((1, cout), lambda i: (0, 0)),
            pl.BlockSpec((1, rb, oh), lambda i: (i, 0, 0)),
            pl.BlockSpec((1, rw, ow), lambda i: (i, 0, 0)),
        ],
        out_specs=pl.BlockSpec((1, rb * rw, cout), lambda i: (i, 0, 0)),
        out_shape=jax.ShapeDtypeStruct((n, rb * rw, cout), jnp.bfloat16),
        scratch_shapes=[pltpu.VMEM((cin // 128, h, wd, 128), jnp.float32)],
        compiler_params=pltpu.CompilerParams(dimension_semantics=("arbitrary",)),
    )(x, w, b.reshape(1, cout), row_mix, col_mix)
    return out.reshape(n, rb, rw, cout)


def shifted(value, axis, steps):
    count = lax.axis_size(axis)
    leading, last = (max(0, -steps), min(count, count - steps))
    return lax.ppermute(value, axis, [(source, source + steps) for source in range(leading, last)])


def with_halo(value, sides, width, wrap):
    for axis, dim in sides:
        size, length = (lax.axis_size(axis), value.shape[dim])
        up = [(i, (i + 1) % size) for i in range(size if wrap else size - 1)]
        down = [(j, i) for i, j in up]
        last = lax.slice_in_dim(value, length - width, length, axis=dim)
        leading = lax.slice_in_dim(value, 0, width, axis=dim)
        before = lax.ppermute(last, axis, up)
        after = lax.ppermute(leading, axis, down)
        value = jnp.concatenate([before, value, after], axis=dim)
    return value


def place_rows(onehot, values):
    shaped = onehot.reshape(onehot.shape + (1,) * (values.ndim - 1))
    return jnp.sum(jnp.where(shaped, values[None], jnp.zeros_like(values[None])), axis=1)


def place_ints(onehot, values):
    return jnp.sum(jnp.where(onehot, values[None, :], 0), axis=1)


def keep_local(keep, values):
    shaped = keep.reshape((keep.shape[0],) + (1,) * (values.ndim - 1))
    return jnp.where(shaped, values, jnp.zeros_like(values))


def depthwise(widened, depth_kernel, height, width):
    mixed = None
    for e in range(KS):
        column = widened[:, e : e + width]
        for a in range(KS):
            term = column[a : a + height] * depth_kernel[a, e]
            mixed = term if mixed is None else mixed + term
    return mixed


def layer_apply(padded, depth_kernel, gain, up_matrix, down_matrix):
    height = padded.shape[0] - (KS - 1)
    width = padded.shape[1] - (KS - 1)
    spare = -width % 8
    widened = padded.astype(jnp.float32)
    if spare:
        widened = jnp.pad(widened, ((0, 0), (0, spare), (0, 0)))
    mixed = depthwise(widened, depth_kernel, height, width + spare)
    centered = mixed - jnp.mean(mixed, axis=-1, keepdims=True)
    variance = jnp.mean(centered * centered, axis=-1, keepdims=True)
    normed = (centered * lax.rsqrt(variance + 1e-06) * gain).astype(jnp.bfloat16)
    flat_cells = normed.reshape(height * (width + spare), -1)
    hidden = jax.nn.gelu(jnp.dot(flat_cells, up_matrix, preferred_element_type=jnp.float32)).astype(
        jnp.bfloat16
    )
    output = jnp.dot(hidden, down_matrix, preferred_element_type=jnp.float32).reshape(
        height, width + spare, -1
    )
    residual_part = widened[HALO : HALO + height, HALO : HALO + width + spare]
    return (residual_part + output).astype(jnp.bfloat16)[:, :width]


def per_device(
    swath_input,
    conv_weight,
    conv_bias,
    block_band,
    row_offset,
    col_offset,
    row_weights,
    col_weights,
    background,
    depth_weight,
    norm_gain,
    up_weight,
    down_weight,
):
    blocks_here = swath_input.shape[0]
    tile_rows = background.shape[0]
    tile_cols = background.shape[1]
    channels = background.shape[2]
    bands = lax.axis_size("lat")
    resampled = conv_resample(swath_input, conv_weight, conv_bias, row_weights, col_weights)
    own_band = lax.axis_index("lat")
    offset_band = block_band[:, 0] - own_band
    staying = offset_band == 0
    positions = jnp.arange(blocks_here, dtype=jnp.int32)
    row_list = [row_offset]
    col_list = [col_offset]
    block_list = [keep_local(staying, resampled)]
    for step in (1, -1):
        going = offset_band == step
        earlier = jnp.sum(going[None, :] & (positions[None, :] < positions[:, None]), axis=1)
        table = (jnp.arange(CAP, dtype=jnp.int32)[:, None] == earlier[None, :]) & going[None, :]
        sent_blocks = place_rows(table, resampled)
        sent_rows = place_ints(table, row_offset)
        sent_cols = place_ints(table, col_offset)
        lane = jnp.arange(channels, dtype=jnp.int32)[None, :]
        header = jnp.where(
            lane == 0, sent_rows[:, None], jnp.where(lane == 1, sent_cols[:, None], 0)
        ).astype(jnp.bfloat16)
        header = jnp.broadcast_to(header[:, None, None, :], (CAP, 1, RW, channels))
        payload = jnp.concatenate([sent_blocks, header], axis=1)
        got = shifted(payload, "lat", step)
        block_list.append(got[:, :RB])
        got_header = got[:, RB, 0, :].astype(jnp.int32)
        row_list.append(got_header[:, 0])
        col_list.append(got_header[:, 1])
    arrived = jnp.concatenate(block_list, axis=0)
    all_rows = jnp.concatenate(row_list, axis=0)
    all_cols = jnp.concatenate(col_list, axis=0)
    row_place = (
        jnp.arange(tile_rows, dtype=jnp.int32)[None, :, None]
        == all_rows[:, None, None] + jnp.arange(RB, dtype=jnp.int32)[None, None, :]
    ).astype(jnp.bfloat16)
    col_place = (
        jnp.arange(tile_cols, dtype=jnp.int32)[None, :, None]
        == all_cols[:, None, None] + jnp.arange(RW, dtype=jnp.int32)[None, None, :]
    ).astype(jnp.bfloat16)
    lifted = jnp.einsum(
        "shr,sruc->shuc", row_place, arrived, preferred_element_type=jnp.float32
    ).astype(jnp.bfloat16)
    summed = jnp.einsum("swu,shuc->hwc", col_place, lifted, preferred_element_type=jnp.float32)
    state = (background.astype(jnp.float32) + summed).astype(jnp.bfloat16)
    reach = HALO * LAYERS
    lon_wide = with_halo(state, (("lon", 1),), reach, True)
    size, length = lax.axis_size("lat"), lon_wide.shape[0]
    up = [(i, i + 1) for i in range(size - 1)]
    down = [(j, i) for i, j in up]
    north = lax.ppermute(lon_wide[length - reach :], "lat", up)
    south = lax.ppermute(lon_wide[:reach], "lat", down)
    first = (
        depth_weight[0],
        norm_gain[0],
        up_weight[0],
        down_weight[0],
    )
    middle = layer_apply(lon_wide, *first)
    top = layer_apply(jnp.concatenate([north, lon_wide[:reach]], axis=0), *first)
    bottom = layer_apply(jnp.concatenate([lon_wide[length - reach :], south], axis=0), *first)
    widened = jnp.concatenate([top, middle, bottom], axis=0)
    first_row = own_band * tile_rows
    margin = (widened.shape[0] - tile_rows) // 2
    grid_row = first_row - margin + jnp.arange(widened.shape[0], dtype=jnp.int32)
    inside = (grid_row >= 0) & (grid_row < bands * tile_rows)
    widened = jnp.where(inside[:, None, None], widened, jnp.zeros_like(widened))
    for layer_index in range(1, LAYERS):
        widened = layer_apply(
            widened,
            depth_weight[layer_index],
            norm_gain[layer_index],
            up_weight[layer_index],
            down_weight[layer_index],
        )
    return widened


def solution(mesh):
    in_specs = (
        P(("lat", "lon"), None, None, None),
        P(),
        P(),
        P(("lat", "lon"), None),
        P(("lat", "lon")),
        P(("lat", "lon")),
        P(("lat", "lon"), None, None),
        P(("lat", "lon"), None, None),
        P("lat", "lon", None),
        P(),
        P(),
        P(),
        P(),
    )
    out_specs = P("lat", "lon", None)
    return jax.shard_map(
        per_device, mesh=mesh, in_specs=in_specs, out_specs=out_specs, check_vma=False
    )
```

```python
import jax
import jax.numpy as jnp
from jax import lax
from jax.experimental import pallas as pl
from jax.experimental.pallas import tpu as pltpu
from jax.sharding import PartitionSpec as P

KS = 7
HALO = 3
LAYERS = 2
CAP = 2
RB = 16
RW = 16


def _expand(count, size, by_block):
    rows = lax.broadcasted_iota(jnp.int32, (count, size), 0)
    cols = lax.broadcasted_iota(jnp.int32, (count, size), 1)
    group = count // size if by_block else 1
    picked = rows // group if by_block else rows % size
    return (picked == cols).astype(jnp.bfloat16)


def _conv_body(x_ref, w_ref, b_ref, r_ref, c_ref, o_ref, wide_ref):
    oh, ow, ch = x_ref.shape[1] // 2, x_ref.shape[2] // 2, o_ref.shape[2]
    cin = x_ref.shape[3]
    lanes = wide_ref.shape[3]
    parts = wide_ref.shape[0]
    for part in range(parts):
        wide_ref[part] = x_ref[0, :, :, part * lanes : (part + 1) * lanes].astype(jnp.float32)

    def parity(rp, cp):
        halves = [
            wide_ref[part, pl.ds(rp, oh, stride=2), pl.ds(cp, ow, stride=2), :].astype(x_ref.dtype)
            for part in range(parts)
        ]
        v = jnp.concatenate(halves, axis=-1)
        return v.reshape(oh * ow, cin)

    def tap(v, a, e):
        return jnp.dot(v, w_ref[a, e], preferred_element_type=jnp.float32)

    even_even, even_odd = parity(0, 0), parity(0, 1)
    odd_even, odd_odd = parity(1, 0), parity(1, 1)
    plain = tap(even_even, 1, 1) + tap(even_odd, 1, 2) + tap(odd_even, 2, 1) + tap(odd_odd, 2, 2)
    row_shift = tap(odd_even, 0, 1) + tap(odd_odd, 0, 2)
    col_shift = tap(even_odd, 1, 0) + tap(odd_odd, 2, 0)
    both_shift = tap(odd_odd, 0, 0)
    plain = plain.reshape(oh, ow, ch)
    row_shift = row_shift.reshape(oh, ow, ch)
    col_shift = col_shift.reshape(oh, ow, ch)
    both_shift = both_shift.reshape(oh, ow, ch)
    zero_row = jnp.zeros((1, ow, ch), jnp.float32)
    col_part = col_shift + jnp.concatenate([zero_row, both_shift[:-1]], axis=0)
    total = plain + jnp.concatenate([zero_row, row_shift[:-1]], axis=0)
    rolled = pltpu.roll(col_part, 1, 1)
    first_col = lax.broadcasted_iota(jnp.int32, (oh, ow, ch), 1) == 0
    total = total + jnp.where(first_col, 0.0, rolled)
    total = total + b_ref[...]
    features = jax.nn.gelu(total).astype(x_ref.dtype).reshape(oh * ow, ch)
    row_mix, col_mix = r_ref[0], c_ref[0]
    rb, rw = row_mix.shape[0], col_mix.shape[0]
    cells = rb * rw
    by_row = jnp.dot(_expand(cells, rb, True), row_mix, preferred_element_type=jnp.float32)
    by_col = jnp.dot(_expand(cells, rw, False), col_mix, preferred_element_type=jnp.float32)
    spread_row = jnp.dot(
        by_row.astype(x_ref.dtype), _expand(oh * ow, oh, True).T, preferred_element_type=jnp.float32
    )
    spread_col = jnp.dot(
        by_col.astype(x_ref.dtype), _expand(oh * ow, ow, False).T, preferred_element_type=jnp.float32
    )
    both = spread_row * spread_col
    high = both.astype(x_ref.dtype)
    low = (both - high.astype(jnp.float32)).astype(x_ref.dtype)
    mixed = jnp.dot(high, features, preferred_element_type=jnp.float32) + jnp.dot(
        low, features, preferred_element_type=jnp.float32
    )
    o_ref[0] = mixed.astype(o_ref.dtype)


def conv_resample(x, w, b, row_mix, col_mix):
    n, h, wd, cin = x.shape
    cout = w.shape[3]
    oh, ow = h // 2, wd // 2
    rb, rw = row_mix.shape[1], col_mix.shape[1]
    out = pl.pallas_call(
        _conv_body,
        grid=(n,),
        in_specs=[
            pl.BlockSpec((1, h, wd, cin), lambda i: (i, 0, 0, 0)),
            pl.BlockSpec((3, 3, cin, cout), lambda i: (0, 0, 0, 0)),
            pl.BlockSpec((1, cout), lambda i: (0, 0)),
            pl.BlockSpec((1, rb, oh), lambda i: (i, 0, 0)),
            pl.BlockSpec((1, rw, ow), lambda i: (i, 0, 0)),
        ],
        out_specs=pl.BlockSpec((1, rb * rw, cout), lambda i: (i, 0, 0)),
        out_shape=jax.ShapeDtypeStruct((n, rb * rw, cout), jnp.bfloat16),
        scratch_shapes=[pltpu.VMEM((cin // 128, h, wd, 128), jnp.float32)],
        compiler_params=pltpu.CompilerParams(dimension_semantics=("arbitrary",)),
    )(x, w, b.reshape(1, cout), row_mix, col_mix)
    return out.reshape(n, rb, rw, cout)


def shifted(value, axis, steps):
    count = lax.axis_size(axis)
    leading, last = (max(0, -steps), min(count, count - steps))
    return lax.ppermute(value, axis, [(source, source + steps) for source in range(leading, last)])


def with_halo(value, sides, width, wrap):
    for axis, dim in sides:
        size, length = (lax.axis_size(axis), value.shape[dim])
        up = [(i, (i + 1) % size) for i in range(size if wrap else size - 1)]
        down = [(j, i) for i, j in up]
        last = lax.slice_in_dim(value, length - width, length, axis=dim)
        leading = lax.slice_in_dim(value, 0, width, axis=dim)
        before = lax.ppermute(last, axis, up)
        after = lax.ppermute(leading, axis, down)
        value = jnp.concatenate([before, value, after], axis=dim)
    return value


def place_rows(onehot, values):
    shaped = onehot.reshape(onehot.shape + (1,) * (values.ndim - 1))
    return jnp.sum(jnp.where(shaped, values[None], jnp.zeros_like(values[None])), axis=1)


def place_ints(onehot, values):
    return jnp.sum(jnp.where(onehot, values[None, :], 0), axis=1)


def keep_local(keep, values):
    shaped = keep.reshape((keep.shape[0],) + (1,) * (values.ndim - 1))
    return jnp.where(shaped, values, jnp.zeros_like(values))


def depthwise(widened, depth_kernel, height, width):
    mixed = None
    for e in range(KS):
        column = widened[:, e : e + width]
        for a in range(KS):
            term = column[a : a + height] * depth_kernel[a, e]
            mixed = term if mixed is None else mixed + term
    return mixed


def layer_apply(padded, depth_kernel, gain, up_matrix, down_matrix):
    height = padded.shape[0] - (KS - 1)
    width = padded.shape[1] - (KS - 1)
    spare = -width % 8
    widened = padded.astype(jnp.float32)
    if spare:
        widened = jnp.pad(widened, ((0, 0), (0, spare), (0, 0)))
    mixed = depthwise(widened, depth_kernel, height, width + spare)
    centered = mixed - jnp.mean(mixed, axis=-1, keepdims=True)
    variance = jnp.mean(centered * centered, axis=-1, keepdims=True)
    normed = (centered * lax.rsqrt(variance + 1e-06) * gain).astype(jnp.bfloat16)
    flat_cells = normed.reshape(height * (width + spare), -1)
    hidden = jax.nn.gelu(jnp.dot(flat_cells, up_matrix, preferred_element_type=jnp.float32)).astype(
        jnp.bfloat16
    )
    output = jnp.dot(hidden, down_matrix, preferred_element_type=jnp.float32).reshape(
        height, width + spare, -1
    )
    residual_part = widened[HALO : HALO + height, HALO : HALO + width + spare]
    return (residual_part + output).astype(jnp.bfloat16)[:, :width]


def per_device(
    swath_input,
    conv_weight,
    conv_bias,
    block_band,
    row_offset,
    col_offset,
    row_weights,
    col_weights,
    background,
    depth_weight,
    norm_gain,
    up_weight,
    down_weight,
):
    blocks_here = swath_input.shape[0]
    tile_rows = background.shape[0]
    tile_cols = background.shape[1]
    channels = background.shape[2]
    bands = lax.axis_size("lat")
    resampled = conv_resample(swath_input, conv_weight, conv_bias, row_weights, col_weights)
    own_band = lax.axis_index("lat")
    offset_band = block_band[:, 0] - own_band
    staying = offset_band == 0
    positions = jnp.arange(blocks_here, dtype=jnp.int32)
    row_list = [row_offset]
    col_list = [col_offset]
    block_list = [keep_local(staying, resampled)]
    for step in (1, -1):
        going = offset_band == step
        earlier = jnp.sum(going[None, :] & (positions[None, :] < positions[:, None]), axis=1)
        table = (jnp.arange(CAP, dtype=jnp.int32)[:, None] == earlier[None, :]) & going[None, :]
        sent_blocks = place_rows(table, resampled)
        sent_rows = place_ints(table, row_offset)
        sent_cols = place_ints(table, col_offset)
        lane = jnp.arange(channels, dtype=jnp.int32)[None, :]
        header = jnp.where(
            lane == 0, sent_rows[:, None], jnp.where(lane == 1, sent_cols[:, None], 0)
        ).astype(jnp.bfloat16)
        header = jnp.broadcast_to(header[:, None, None, :], (CAP, 1, RW, channels))
        payload = jnp.concatenate([sent_blocks, header], axis=1)
        got = shifted(payload, "lat", step)
        block_list.append(got[:, :RB])
        got_header = got[:, RB, 0, :].astype(jnp.int32)
        row_list.append(got_header[:, 0])
        col_list.append(got_header[:, 1])
    arrived = jnp.concatenate(block_list, axis=0)
    all_rows = jnp.concatenate(row_list, axis=0)
    all_cols = jnp.concatenate(col_list, axis=0)
    row_place = (
        jnp.arange(tile_rows, dtype=jnp.int32)[None, :, None]
        == all_rows[:, None, None] + jnp.arange(RB, dtype=jnp.int32)[None, None, :]
    ).astype(jnp.bfloat16)
    col_place = (
        jnp.arange(tile_cols, dtype=jnp.int32)[None, :, None]
        == all_cols[:, None, None] + jnp.arange(RW, dtype=jnp.int32)[None, None, :]
    ).astype(jnp.bfloat16)
    lifted = jnp.einsum(
        "shr,sruc->shuc", row_place, arrived, preferred_element_type=jnp.float32
    ).astype(jnp.bfloat16)
    summed = jnp.einsum("swu,shuc->hwc", col_place, lifted, preferred_element_type=jnp.float32)
    state = (background.astype(jnp.float32) + summed).astype(jnp.bfloat16)
    reach = HALO * LAYERS
    lon_wide = with_halo(state, (("lon", 1),), reach, True)
    size, length = lax.axis_size("lat"), lon_wide.shape[0]
    up = [(i, i + 1) for i in range(size - 1)]
    down = [(j, i) for i, j in up]
    north = lax.ppermute(lon_wide[length - reach :], "lat", up)
    south = lax.ppermute(lon_wide[:reach], "lat", down)
    first = (
        depth_weight[0],
        norm_gain[0],
        up_weight[0],
        down_weight[0],
    )
    inner = layer_apply(state, *first)
    west_part = layer_apply(lon_wide[:, : 4 * HALO], *first)
    east_part = layer_apply(lon_wide[:, lon_wide.shape[1] - 4 * HALO :], *first)
    middle = jnp.concatenate([west_part, inner, east_part], axis=1)
    top = layer_apply(jnp.concatenate([north, lon_wide[:reach]], axis=0), *first)
    bottom = layer_apply(jnp.concatenate([lon_wide[length - reach :], south], axis=0), *first)
    widened = jnp.concatenate([top, middle, bottom], axis=0)
    first_row = own_band * tile_rows
    margin = (widened.shape[0] - tile_rows) // 2
    grid_row = first_row - margin + jnp.arange(widened.shape[0], dtype=jnp.int32)
    inside = (grid_row >= 0) & (grid_row < bands * tile_rows)
    widened = jnp.where(inside[:, None, None], widened, jnp.zeros_like(widened))
    for layer_index in range(1, LAYERS):
        widened = layer_apply(
            widened,
            depth_weight[layer_index],
            norm_gain[layer_index],
            up_weight[layer_index],
            down_weight[layer_index],
        )
    return widened


def solution(mesh):
    in_specs = (
        P(("lat", "lon"), None, None, None),
        P(),
        P(),
        P(("lat", "lon"), None),
        P(("lat", "lon")),
        P(("lat", "lon")),
        P(("lat", "lon"), None, None),
        P(("lat", "lon"), None, None),
        P("lat", "lon", None),
        P(),
        P(),
        P(),
        P(),
    )
    out_specs = P("lat", "lon", None)
    return jax.shard_map(
        per_device, mesh=mesh, in_specs=in_specs, out_specs=out_specs, check_vma=False
    )
```

```python
import jax
import jax.numpy as jnp
from jax import lax
from jax.experimental import pallas as pl
from jax.experimental.pallas import tpu as pltpu
from jax.sharding import PartitionSpec as P

KS = 7
HALO = 3
LAYERS = 2
CAP = 2
RB = 16
RW = 16


def _expand(count, size, by_block):
    rows = lax.broadcasted_iota(jnp.int32, (count, size), 0)
    cols = lax.broadcasted_iota(jnp.int32, (count, size), 1)
    group = count // size if by_block else 1
    picked = rows // group if by_block else rows % size
    return (picked == cols).astype(jnp.bfloat16)


def _conv_body(x_ref, w_ref, b_ref, r_ref, c_ref, o_ref, wide_ref):
    oh, ow, ch = x_ref.shape[1] // 2, x_ref.shape[2] // 2, o_ref.shape[2]
    cin = x_ref.shape[3]
    lanes = wide_ref.shape[3]
    parts = wide_ref.shape[0]
    for part in range(parts):
        wide_ref[part] = x_ref[0, :, :, part * lanes : (part + 1) * lanes].astype(jnp.float32)

    def parity(rp, cp):
        halves = [
            wide_ref[part, pl.ds(rp, oh, stride=2), pl.ds(cp, ow, stride=2), :].astype(x_ref.dtype)
            for part in range(parts)
        ]
        v = jnp.concatenate(halves, axis=-1)
        return v.reshape(oh * ow, cin)

    def tap(v, a, e):
        return jnp.dot(v, w_ref[a, e], preferred_element_type=jnp.float32)

    even_even, even_odd = parity(0, 0), parity(0, 1)
    odd_even, odd_odd = parity(1, 0), parity(1, 1)
    plain = tap(even_even, 1, 1) + tap(even_odd, 1, 2) + tap(odd_even, 2, 1) + tap(odd_odd, 2, 2)
    row_shift = tap(odd_even, 0, 1) + tap(odd_odd, 0, 2)
    col_shift = tap(even_odd, 1, 0) + tap(odd_odd, 2, 0)
    both_shift = tap(odd_odd, 0, 0)
    plain = plain.reshape(oh, ow, ch)
    row_shift = row_shift.reshape(oh, ow, ch)
    col_shift = col_shift.reshape(oh, ow, ch)
    both_shift = both_shift.reshape(oh, ow, ch)
    zero_row = jnp.zeros((1, ow, ch), jnp.float32)
    col_part = col_shift + jnp.concatenate([zero_row, both_shift[:-1]], axis=0)
    total = plain + jnp.concatenate([zero_row, row_shift[:-1]], axis=0)
    rolled = pltpu.roll(col_part, 1, 1)
    first_col = lax.broadcasted_iota(jnp.int32, (oh, ow, ch), 1) == 0
    total = total + jnp.where(first_col, 0.0, rolled)
    total = total + b_ref[...]
    features = jax.nn.gelu(total).astype(x_ref.dtype).reshape(oh * ow, ch)
    row_mix, col_mix = r_ref[0], c_ref[0]
    rb, rw = row_mix.shape[0], col_mix.shape[0]
    cells = rb * rw
    by_row = jnp.dot(_expand(cells, rb, True), row_mix, preferred_element_type=jnp.float32)
    by_col = jnp.dot(_expand(cells, rw, False), col_mix, preferred_element_type=jnp.float32)
    spread_row = jnp.dot(
        by_row.astype(x_ref.dtype), _expand(oh * ow, oh, True).T, preferred_element_type=jnp.float32
    )
    spread_col = jnp.dot(
        by_col.astype(x_ref.dtype), _expand(oh * ow, ow, False).T, preferred_element_type=jnp.float32
    )
    both = spread_row * spread_col
    high = both.astype(x_ref.dtype)
    low = (both - high.astype(jnp.float32)).astype(x_ref.dtype)
    mixed = jnp.dot(high, features, preferred_element_type=jnp.float32) + jnp.dot(
        low, features, preferred_element_type=jnp.float32
    )
    o_ref[0] = mixed.astype(o_ref.dtype)


def conv_resample(x, w, b, row_mix, col_mix):
    n, h, wd, cin = x.shape
    cout = w.shape[3]
    oh, ow = h // 2, wd // 2
    rb, rw = row_mix.shape[1], col_mix.shape[1]
    out = pl.pallas_call(
        _conv_body,
        grid=(n,),
        in_specs=[
            pl.BlockSpec((1, h, wd, cin), lambda i: (i, 0, 0, 0)),
            pl.BlockSpec((3, 3, cin, cout), lambda i: (0, 0, 0, 0)),
            pl.BlockSpec((1, cout), lambda i: (0, 0)),
            pl.BlockSpec((1, rb, oh), lambda i: (i, 0, 0)),
            pl.BlockSpec((1, rw, ow), lambda i: (i, 0, 0)),
        ],
        out_specs=pl.BlockSpec((1, rb * rw, cout), lambda i: (i, 0, 0)),
        out_shape=jax.ShapeDtypeStruct((n, rb * rw, cout), jnp.bfloat16),
        scratch_shapes=[pltpu.VMEM((cin // 128, h, wd, 128), jnp.float32)],
        compiler_params=pltpu.CompilerParams(dimension_semantics=("arbitrary",)),
    )(x, w, b.reshape(1, cout), row_mix, col_mix)
    return out.reshape(n, rb, rw, cout)


def shifted(value, axis, steps):
    count = lax.axis_size(axis)
    leading, last = (max(0, -steps), min(count, count - steps))
    return lax.ppermute(value, axis, [(source, source + steps) for source in range(leading, last)])


def with_halo(value, sides, width, wrap):
    for axis, dim in sides:
        size, length = (lax.axis_size(axis), value.shape[dim])
        up = [(i, (i + 1) % size) for i in range(size if wrap else size - 1)]
        down = [(j, i) for i, j in up]
        last = lax.slice_in_dim(value, length - width, length, axis=dim)
        leading = lax.slice_in_dim(value, 0, width, axis=dim)
        before = lax.ppermute(last, axis, up)
        after = lax.ppermute(leading, axis, down)
        value = jnp.concatenate([before, value, after], axis=dim)
    return value


def place_rows(onehot, values):
    shaped = onehot.reshape(onehot.shape + (1,) * (values.ndim - 1))
    return jnp.sum(jnp.where(shaped, values[None], jnp.zeros_like(values[None])), axis=1)


def place_ints(onehot, values):
    return jnp.sum(jnp.where(onehot, values[None, :], 0), axis=1)


def keep_local(keep, values):
    shaped = keep.reshape((keep.shape[0],) + (1,) * (values.ndim - 1))
    return jnp.where(shaped, values, jnp.zeros_like(values))


def depthwise(widened, depth_kernel, height, width):
    mixed = None
    for e in range(KS):
        column = widened[..., e : e + width, :]
        for a in range(KS):
            term = column[..., a : a + height, :, :] * depth_kernel[a, e]
            mixed = term if mixed is None else mixed + term
    return mixed


def layer_apply(padded, depth_kernel, gain, up_matrix, down_matrix):
    height = padded.shape[-3] - (KS - 1)
    width = padded.shape[-2] - (KS - 1)
    spare = -width % 8
    widened = padded.astype(jnp.float32)
    if spare:
        widened = jnp.pad(widened, [(0, 0)] * (widened.ndim - 2) + [(0, spare), (0, 0)])
    mixed = depthwise(widened, depth_kernel, height, width + spare)
    centered = mixed - jnp.mean(mixed, axis=-1, keepdims=True)
    variance = jnp.mean(centered * centered, axis=-1, keepdims=True)
    normed = (centered * lax.rsqrt(variance + 1e-06) * gain).astype(jnp.bfloat16)
    flat_cells = normed.reshape(-1, normed.shape[-1])
    hidden = jax.nn.gelu(jnp.dot(flat_cells, up_matrix, preferred_element_type=jnp.float32)).astype(
        jnp.bfloat16
    )
    output = jnp.dot(hidden, down_matrix, preferred_element_type=jnp.float32).reshape(normed.shape)
    residual_part = widened[..., HALO : HALO + height, HALO : HALO + width + spare, :]
    return (residual_part + output).astype(jnp.bfloat16)[..., :width, :]


def per_device(
    swath_input,
    conv_weight,
    conv_bias,
    block_band,
    row_offset,
    col_offset,
    row_weights,
    col_weights,
    background,
    depth_weight,
    norm_gain,
    up_weight,
    down_weight,
):
    blocks_here = swath_input.shape[0]
    tile_rows = background.shape[0]
    tile_cols = background.shape[1]
    channels = background.shape[2]
    bands = lax.axis_size("lat")
    resampled = conv_resample(swath_input, conv_weight, conv_bias, row_weights, col_weights)
    own_band = lax.axis_index("lat")
    offset_band = block_band[:, 0] - own_band
    staying = offset_band == 0
    positions = jnp.arange(blocks_here, dtype=jnp.int32)
    row_list = [row_offset]
    col_list = [col_offset]
    block_list = [keep_local(staying, resampled)]
    for step in (1, -1):
        going = offset_band == step
        earlier = jnp.sum(going[None, :] & (positions[None, :] < positions[:, None]), axis=1)
        table = (jnp.arange(CAP, dtype=jnp.int32)[:, None] == earlier[None, :]) & going[None, :]
        sent_blocks = place_rows(table, resampled)
        sent_rows = place_ints(table, row_offset)
        sent_cols = place_ints(table, col_offset)
        lane = jnp.arange(channels, dtype=jnp.int32)[None, :]
        header = jnp.where(
            lane == 0, sent_rows[:, None], jnp.where(lane == 1, sent_cols[:, None], 0)
        ).astype(jnp.bfloat16)
        header = jnp.broadcast_to(header[:, None, None, :], (CAP, 1, RW, channels))
        payload = jnp.concatenate([sent_blocks, header], axis=1)
        got = shifted(payload, "lat", step)
        block_list.append(got[:, :RB])
        got_header = got[:, RB, 0, :].astype(jnp.int32)
        row_list.append(got_header[:, 0])
        col_list.append(got_header[:, 1])
    arrived = jnp.concatenate(block_list, axis=0)
    all_rows = jnp.concatenate(row_list, axis=0)
    all_cols = jnp.concatenate(col_list, axis=0)
    row_place = (
        jnp.arange(tile_rows, dtype=jnp.int32)[None, :, None]
        == all_rows[:, None, None] + jnp.arange(RB, dtype=jnp.int32)[None, None, :]
    ).astype(jnp.bfloat16)
    col_place = (
        jnp.arange(tile_cols, dtype=jnp.int32)[None, :, None]
        == all_cols[:, None, None] + jnp.arange(RW, dtype=jnp.int32)[None, None, :]
    ).astype(jnp.bfloat16)
    lifted = jnp.einsum(
        "shr,sruc->shuc", row_place, arrived, preferred_element_type=jnp.float32
    ).astype(jnp.bfloat16)
    summed = jnp.einsum("swu,shuc->hwc", col_place, lifted, preferred_element_type=jnp.float32)
    state = (background.astype(jnp.float32) + summed).astype(jnp.bfloat16)
    reach = HALO * LAYERS
    lon_wide = with_halo(state, (("lon", 1),), reach, True)
    size, length = lax.axis_size("lat"), lon_wide.shape[0]
    up = [(i, i + 1) for i in range(size - 1)]
    down = [(j, i) for i, j in up]
    north = lax.ppermute(lon_wide[length - reach :], "lat", up)
    south = lax.ppermute(lon_wide[:reach], "lat", down)
    first = (depth_weight[0], norm_gain[0], up_weight[0], down_weight[0])
    second = (depth_weight[1], norm_gain[1], up_weight[1], down_weight[1])
    middle = layer_apply(lon_wide, *first)
    later_middle = layer_apply(middle, *second)
    edges = jnp.stack(
        [
            jnp.concatenate([north, lon_wide[:reach]], axis=0),
            jnp.concatenate([lon_wide[length - reach :], south], axis=0),
        ]
    )
    outer = layer_apply(edges, *first)
    first_row = own_band * tile_rows
    outer_rows = jnp.stack(
        [
            first_row - HALO + jnp.arange(reach, dtype=jnp.int32),
            first_row + tile_rows + HALO - reach + jnp.arange(reach, dtype=jnp.int32),
        ]
    )
    inside = (outer_rows >= 0) & (outer_rows < bands * tile_rows)
    outer = jnp.where(inside[:, :, None, None], outer, jnp.zeros_like(outer))
    later_edges = jnp.stack(
        [
            jnp.concatenate([outer[0], middle[:reach]], axis=0),
            jnp.concatenate([middle[middle.shape[0] - reach :], outer[1]], axis=0),
        ]
    )
    later_outer = layer_apply(later_edges, *second)
    widened = jnp.concatenate([later_outer[0], later_middle, later_outer[1]], axis=0)
    return widened


def solution(mesh):
    in_specs = (
        P(("lat", "lon"), None, None, None),
        P(),
        P(),
        P(("lat", "lon"), None),
        P(("lat", "lon")),
        P(("lat", "lon")),
        P(("lat", "lon"), None, None),
        P(("lat", "lon"), None, None),
        P("lat", "lon", None),
        P(),
        P(),
        P(),
        P(),
    )
    out_specs = P("lat", "lon", None)
    return jax.shard_map(
        per_device, mesh=mesh, in_specs=in_specs, out_specs=out_specs, check_vma=False
    )
```

```python
import jax
import jax.numpy as jnp
from jax import lax
from jax.experimental import pallas as pl
from jax.experimental.pallas import tpu as pltpu
from jax.sharding import PartitionSpec as P

KS = 7
HALO = 3
LAYERS = 2
CAP = 2
RB = 16
RW = 16


def _expand(count, size, by_block, across=False):
    shape = (size, count) if across else (count, size)
    rows = lax.broadcasted_iota(jnp.int32, shape, 1 if across else 0)
    cols = lax.broadcasted_iota(jnp.int32, shape, 0 if across else 1)
    group = count // size if by_block else 1
    picked = rows // group if by_block else rows % size
    return (picked == cols).astype(jnp.bfloat16)


def _conv_body(x_ref, w_ref, b_ref, r_ref, c_ref, o_ref, wide_ref):
    oh, ow, ch = x_ref.shape[1] // 2, x_ref.shape[2] // 2, o_ref.shape[2]
    cin = x_ref.shape[3]
    lanes = wide_ref.shape[3]
    parts = wide_ref.shape[0]
    for part in range(parts):
        wide_ref[part] = x_ref[0, :, :, part * lanes : (part + 1) * lanes].astype(jnp.float32)

    def parity(rp, cp):
        halves = [
            wide_ref[part, pl.ds(rp, oh, stride=2), pl.ds(cp, ow, stride=2), :].astype(x_ref.dtype)
            for part in range(parts)
        ]
        v = jnp.concatenate(halves, axis=-1)
        return v.reshape(oh * ow, cin)

    def tap(v, a, e):
        return jnp.dot(v, w_ref[a, e], preferred_element_type=jnp.float32)

    even_even, even_odd = parity(0, 0), parity(0, 1)
    odd_even, odd_odd = parity(1, 0), parity(1, 1)
    plain = tap(even_even, 1, 1) + tap(even_odd, 1, 2) + tap(odd_even, 2, 1) + tap(odd_odd, 2, 2)
    row_shift = tap(odd_even, 0, 1) + tap(odd_odd, 0, 2)
    col_shift = tap(even_odd, 1, 0) + tap(odd_odd, 2, 0)
    both_shift = tap(odd_odd, 0, 0)
    plain = plain.reshape(oh, ow, ch)
    row_shift = row_shift.reshape(oh, ow, ch)
    col_shift = col_shift.reshape(oh, ow, ch)
    both_shift = both_shift.reshape(oh, ow, ch)
    zero_row = jnp.zeros((1, ow, ch), jnp.float32)
    col_part = col_shift + jnp.concatenate([zero_row, both_shift[:-1]], axis=0)
    total = plain + jnp.concatenate([zero_row, row_shift[:-1]], axis=0)
    rolled = pltpu.roll(col_part, 1, 1)
    first_col = lax.broadcasted_iota(jnp.int32, (oh, ow, ch), 1) == 0
    total = total + jnp.where(first_col, 0.0, rolled)
    total = total + b_ref[...]
    features = jax.nn.gelu(total).astype(x_ref.dtype).reshape(oh * ow, ch)
    row_mix, col_mix = r_ref[0], c_ref[0]
    rb, rw = row_mix.shape[0], col_mix.shape[0]
    cells = rb * rw
    by_row = jnp.dot(_expand(cells, rb, True), row_mix, preferred_element_type=jnp.float32)
    by_col = jnp.dot(_expand(cells, rw, False), col_mix, preferred_element_type=jnp.float32)
    spread_row = jnp.dot(
        by_row.astype(x_ref.dtype), _expand(oh * ow, oh, True, True), preferred_element_type=jnp.float32
    )
    spread_col = jnp.dot(
        by_col.astype(x_ref.dtype), _expand(oh * ow, ow, False, True), preferred_element_type=jnp.float32
    )
    both = spread_row * spread_col
    high = both.astype(x_ref.dtype)
    low = (both - high.astype(jnp.float32)).astype(x_ref.dtype)
    mixed = jnp.dot(high, features, preferred_element_type=jnp.float32) + jnp.dot(
        low, features, preferred_element_type=jnp.float32
    )
    o_ref[0] = mixed.astype(o_ref.dtype)


def conv_resample(x, w, b, row_mix, col_mix):
    n, h, wd, cin = x.shape
    cout = w.shape[3]
    oh, ow = h // 2, wd // 2
    rb, rw = row_mix.shape[1], col_mix.shape[1]
    out = pl.pallas_call(
        _conv_body,
        grid=(n,),
        in_specs=[
            pl.BlockSpec((1, h, wd, cin), lambda i: (i, 0, 0, 0)),
            pl.BlockSpec((3, 3, cin, cout), lambda i: (0, 0, 0, 0)),
            pl.BlockSpec((1, cout), lambda i: (0, 0)),
            pl.BlockSpec((1, rb, oh), lambda i: (i, 0, 0)),
            pl.BlockSpec((1, rw, ow), lambda i: (i, 0, 0)),
        ],
        out_specs=pl.BlockSpec((1, rb * rw, cout), lambda i: (i, 0, 0)),
        out_shape=jax.ShapeDtypeStruct((n, rb * rw, cout), jnp.bfloat16),
        scratch_shapes=[pltpu.VMEM((cin // 128, h, wd, 128), jnp.float32)],
        compiler_params=pltpu.CompilerParams(dimension_semantics=("arbitrary",)),
    )(x, w, b.reshape(1, cout), row_mix, col_mix)
    return out.reshape(n, rb, rw, cout)


def shifted(value, axis, steps):
    count = lax.axis_size(axis)
    leading, last = (max(0, -steps), min(count, count - steps))
    return lax.ppermute(value, axis, [(source, source + steps) for source in range(leading, last)])


def with_halo(value, sides, width, wrap):
    for axis, dim in sides:
        size, length = (lax.axis_size(axis), value.shape[dim])
        up = [(i, (i + 1) % size) for i in range(size if wrap else size - 1)]
        down = [(j, i) for i, j in up]
        last = lax.slice_in_dim(value, length - width, length, axis=dim)
        leading = lax.slice_in_dim(value, 0, width, axis=dim)
        before = lax.ppermute(last, axis, up)
        after = lax.ppermute(leading, axis, down)
        value = jnp.concatenate([before, value, after], axis=dim)
    return value


def place_rows(onehot, values):
    flat_values = values.reshape(values.shape[0], -1)
    placed = jnp.dot(onehot.astype(values.dtype), flat_values, preferred_element_type=jnp.float32)
    return placed.astype(values.dtype).reshape((onehot.shape[0],) + values.shape[1:])


def place_ints(onehot, values):
    return jnp.sum(jnp.where(onehot, values[None, :], 0), axis=1)


def keep_local(keep, values):
    shaped = keep.reshape((keep.shape[0],) + (1,) * (values.ndim - 1))
    return jnp.where(shaped, values, jnp.zeros_like(values))


def depthwise(widened, depth_kernel, height, width):
    mixed = None
    for e in range(KS):
        column = widened[:, e : e + width]
        for a in range(KS):
            term = column[a : a + height] * depth_kernel[a, e]
            mixed = term if mixed is None else mixed + term
    return mixed


def layer_apply(padded, depth_kernel, gain, up_matrix, down_matrix):
    height = padded.shape[0] - (KS - 1)
    width = padded.shape[1] - (KS - 1)
    spare = -width % 8
    widened = padded.astype(jnp.float32)
    if spare:
        widened = jnp.pad(widened, ((0, 0), (0, spare), (0, 0)))
    mixed = depthwise(widened, depth_kernel, height, width + spare)
    centered = mixed - jnp.mean(mixed, axis=-1, keepdims=True)
    variance = jnp.mean(centered * centered, axis=-1, keepdims=True)
    normed = (centered * lax.rsqrt(variance + 1e-06) * gain).astype(jnp.bfloat16)
    flat_cells = normed.reshape(height * (width + spare), -1)
    hidden = jax.nn.gelu(jnp.dot(flat_cells, up_matrix, preferred_element_type=jnp.float32)).astype(
        jnp.bfloat16
    )
    output = jnp.dot(hidden, down_matrix, preferred_element_type=jnp.float32).reshape(
        height, width + spare, -1
    )
    residual_part = widened[HALO : HALO + height, HALO : HALO + width + spare]
    return (residual_part + output).astype(jnp.bfloat16)[:, :width]


def per_device(
    swath_input,
    conv_weight,
    conv_bias,
    block_band,
    row_offset,
    col_offset,
    row_weights,
    col_weights,
    background,
    depth_weight,
    norm_gain,
    up_weight,
    down_weight,
):
    blocks_here = swath_input.shape[0]
    tile_rows = background.shape[0]
    tile_cols = background.shape[1]
    channels = background.shape[2]
    bands = lax.axis_size("lat")
    resampled = conv_resample(swath_input, conv_weight, conv_bias, row_weights, col_weights)
    own_band = lax.axis_index("lat")
    offset_band = block_band[:, 0] - own_band
    staying = offset_band == 0
    positions = jnp.arange(blocks_here, dtype=jnp.int32)
    row_list = [row_offset]
    col_list = [col_offset]
    block_list = [keep_local(staying, resampled)]
    for step in (1, -1):
        going = offset_band == step
        earlier = jnp.sum(going[None, :] & (positions[None, :] < positions[:, None]), axis=1)
        table = (jnp.arange(CAP, dtype=jnp.int32)[:, None] == earlier[None, :]) & going[None, :]
        sent_blocks = place_rows(table, resampled)
        sent_rows = place_ints(table, row_offset)
        sent_cols = place_ints(table, col_offset)
        lane = jnp.arange(channels, dtype=jnp.int32)[None, :]
        header = jnp.where(
            lane == 0, sent_rows[:, None], jnp.where(lane == 1, sent_cols[:, None], 0)
        ).astype(jnp.bfloat16)
        header = jnp.broadcast_to(header[:, None, None, :], (CAP, 1, RW, channels))
        payload = jnp.concatenate([sent_blocks, header], axis=1)
        got = shifted(payload, "lat", step)
        block_list.append(got[:, :RB])
        got_header = got[:, RB, 0, :].astype(jnp.int32)
        row_list.append(got_header[:, 0])
        col_list.append(got_header[:, 1])
    arrived = jnp.concatenate(block_list, axis=0)
    all_rows = jnp.concatenate(row_list, axis=0)
    all_cols = jnp.concatenate(col_list, axis=0)
    row_place = (
        jnp.arange(tile_rows, dtype=jnp.int32)[None, :, None]
        == all_rows[:, None, None] + jnp.arange(RB, dtype=jnp.int32)[None, None, :]
    ).astype(jnp.bfloat16)
    col_place = (
        jnp.arange(tile_cols, dtype=jnp.int32)[None, :, None]
        == all_cols[:, None, None] + jnp.arange(RW, dtype=jnp.int32)[None, None, :]
    ).astype(jnp.bfloat16)
    lifted = jnp.einsum(
        "shr,sruc->shuc", row_place, arrived, preferred_element_type=jnp.float32
    ).astype(jnp.bfloat16)
    summed = jnp.einsum("swu,shuc->hwc", col_place, lifted, preferred_element_type=jnp.float32)
    state = (background.astype(jnp.float32) + summed).astype(jnp.bfloat16)
    reach = HALO * LAYERS
    lon_wide = with_halo(state, (("lon", 1),), reach, True)
    size, length = lax.axis_size("lat"), lon_wide.shape[0]
    up = [(i, i + 1) for i in range(size - 1)]
    down = [(j, i) for i, j in up]
    north = lax.ppermute(lon_wide[length - reach :], "lat", up)
    south = lax.ppermute(lon_wide[:reach], "lat", down)
    first = (
        depth_weight[0],
        norm_gain[0],
        up_weight[0],
        down_weight[0],
    )
    middle = layer_apply(lon_wide, *first)
    top = layer_apply(jnp.concatenate([north, lon_wide[:reach]], axis=0), *first)
    bottom = layer_apply(jnp.concatenate([lon_wide[length - reach :], south], axis=0), *first)
    widened = jnp.concatenate([top, middle, bottom], axis=0)
    first_row = own_band * tile_rows
    margin = (widened.shape[0] - tile_rows) // 2
    grid_row = first_row - margin + jnp.arange(widened.shape[0], dtype=jnp.int32)
    inside = (grid_row >= 0) & (grid_row < bands * tile_rows)
    widened = jnp.where(inside[:, None, None], widened, jnp.zeros_like(widened))
    for layer_index in range(1, LAYERS):
        widened = layer_apply(
            widened,
            depth_weight[layer_index],
            norm_gain[layer_index],
            up_weight[layer_index],
            down_weight[layer_index],
        )
    return widened


def solution(mesh):
    in_specs = (
        P(("lat", "lon"), None, None, None),
        P(),
        P(),
        P(("lat", "lon"), None),
        P(("lat", "lon")),
        P(("lat", "lon")),
        P(("lat", "lon"), None, None),
        P(("lat", "lon"), None, None),
        P("lat", "lon", None),
        P(),
        P(),
        P(),
        P(),
    )
    out_specs = P("lat", "lon", None)
    return jax.shard_map(
        per_device, mesh=mesh, in_specs=in_specs, out_specs=out_specs, check_vma=False
    )
```

```python
import jax
import jax.numpy as jnp
from jax import lax
from jax.experimental import pallas as pl
from jax.experimental.pallas import tpu as pltpu
from jax.sharding import PartitionSpec as P

KS = 7
HALO = 3
LAYERS = 2
CAP = 2
RB = 16
RW = 16


def _expand(count, size, by_block, across=False):
    shape = (size, count) if across else (count, size)
    rows = lax.broadcasted_iota(jnp.int32, shape, 1 if across else 0)
    cols = lax.broadcasted_iota(jnp.int32, shape, 0 if across else 1)
    group = count // size if by_block else 1
    picked = rows // group if by_block else rows % size
    return (picked == cols).astype(jnp.bfloat16)


def _conv_body(x_ref, w_ref, b_ref, r_ref, c_ref, o_ref, wide_ref):
    oh, ow, ch = x_ref.shape[1] // 2, x_ref.shape[2] // 2, o_ref.shape[2]
    cin = x_ref.shape[3]
    lanes = wide_ref.shape[3]
    parts = wide_ref.shape[0]
    for part in range(parts):
        wide_ref[part] = x_ref[0, :, :, part * lanes : (part + 1) * lanes].astype(jnp.float32)

    def parity(rp, cp):
        halves = [
            wide_ref[part, pl.ds(rp, oh, stride=2), pl.ds(cp, ow, stride=2), :].astype(x_ref.dtype)
            for part in range(parts)
        ]
        v = jnp.concatenate(halves, axis=-1)
        return v.reshape(oh * ow, cin)

    def tap(v, a, e):
        return jnp.dot(v, w_ref[a, e], preferred_element_type=jnp.float32)

    even_even, even_odd = parity(0, 0), parity(0, 1)
    odd_even, odd_odd = parity(1, 0), parity(1, 1)
    plain = tap(even_even, 1, 1) + tap(even_odd, 1, 2) + tap(odd_even, 2, 1) + tap(odd_odd, 2, 2)
    row_shift = tap(odd_even, 0, 1) + tap(odd_odd, 0, 2)
    col_shift = tap(even_odd, 1, 0) + tap(odd_odd, 2, 0)
    both_shift = tap(odd_odd, 0, 0)
    plain = plain.reshape(oh, ow, ch)
    row_shift = row_shift.reshape(oh, ow, ch)
    col_shift = col_shift.reshape(oh, ow, ch)
    both_shift = both_shift.reshape(oh, ow, ch)
    zero_row = jnp.zeros((1, ow, ch), jnp.float32)
    col_part = col_shift + jnp.concatenate([zero_row, both_shift[:-1]], axis=0)
    total = plain + jnp.concatenate([zero_row, row_shift[:-1]], axis=0)
    rolled = pltpu.roll(col_part, 1, 1)
    first_col = lax.broadcasted_iota(jnp.int32, (oh, ow, ch), 1) == 0
    total = total + jnp.where(first_col, 0.0, rolled)
    total = total + b_ref[...]
    features = jax.nn.gelu(total).astype(x_ref.dtype).reshape(oh * ow, ch)
    row_mix, col_mix = r_ref[0], c_ref[0]
    rb, rw = row_mix.shape[0], col_mix.shape[0]
    cells = rb * rw
    by_row = jnp.dot(_expand(cells, rb, True), row_mix, preferred_element_type=jnp.float32)
    by_col = jnp.dot(_expand(cells, rw, False), col_mix, preferred_element_type=jnp.float32)
    spread_row = jnp.dot(
        by_row.astype(x_ref.dtype), _expand(oh * ow, oh, True, True), preferred_element_type=jnp.float32
    )
    spread_col = jnp.dot(
        by_col.astype(x_ref.dtype), _expand(oh * ow, ow, False, True), preferred_element_type=jnp.float32
    )
    both = spread_row * spread_col
    high = both.astype(x_ref.dtype)
    low = (both - high.astype(jnp.float32)).astype(x_ref.dtype)
    mixed = jnp.dot(high, features, preferred_element_type=jnp.float32) + jnp.dot(
        low, features, preferred_element_type=jnp.float32
    )
    o_ref[0] = mixed.astype(o_ref.dtype)


def conv_resample(x, w, b, row_mix, col_mix):
    n, h, wd, cin = x.shape
    cout = w.shape[3]
    oh, ow = h // 2, wd // 2
    rb, rw = row_mix.shape[1], col_mix.shape[1]
    out = pl.pallas_call(
        _conv_body,
        grid=(n,),
        in_specs=[
            pl.BlockSpec((1, h, wd, cin), lambda i: (i, 0, 0, 0)),
            pl.BlockSpec((3, 3, cin, cout), lambda i: (0, 0, 0, 0)),
            pl.BlockSpec((1, cout), lambda i: (0, 0)),
            pl.BlockSpec((1, rb, oh), lambda i: (i, 0, 0)),
            pl.BlockSpec((1, rw, ow), lambda i: (i, 0, 0)),
        ],
        out_specs=pl.BlockSpec((1, rb * rw, cout), lambda i: (i, 0, 0)),
        out_shape=jax.ShapeDtypeStruct((n, rb * rw, cout), jnp.bfloat16),
        scratch_shapes=[pltpu.VMEM((cin // 128, h, wd, 128), jnp.float32)],
        compiler_params=pltpu.CompilerParams(dimension_semantics=("arbitrary",)),
    )(x, w, b.reshape(1, cout), row_mix, col_mix)
    return out.reshape(n, rb, rw, cout)


def shifted(value, axis, steps):
    count = lax.axis_size(axis)
    leading, last = (max(0, -steps), min(count, count - steps))
    return lax.ppermute(value, axis, [(source, source + steps) for source in range(leading, last)])


def with_halo(value, sides, width, wrap):
    for axis, dim in sides:
        size, length = (lax.axis_size(axis), value.shape[dim])
        up = [(i, (i + 1) % size) for i in range(size if wrap else size - 1)]
        down = [(j, i) for i, j in up]
        last = lax.slice_in_dim(value, length - width, length, axis=dim)
        leading = lax.slice_in_dim(value, 0, width, axis=dim)
        before = lax.ppermute(last, axis, up)
        after = lax.ppermute(leading, axis, down)
        value = jnp.concatenate([before, value, after], axis=dim)
    return value


def place_rows(onehot, values):
    flat_values = values.reshape(values.shape[0], -1)
    placed = jnp.dot(onehot.astype(values.dtype), flat_values, preferred_element_type=jnp.float32)
    return placed.astype(values.dtype).reshape((onehot.shape[0],) + values.shape[1:])


def place_ints(onehot, values):
    return jnp.sum(jnp.where(onehot, values[None, :], 0), axis=1)


def keep_local(keep, values):
    shaped = keep.reshape((keep.shape[0],) + (1,) * (values.ndim - 1))
    return jnp.where(shaped, values, jnp.zeros_like(values))


def depthwise(widened, depth_kernel, height, width):
    mixed = None
    for e in range(KS):
        column = widened[:, e : e + width]
        for a in range(KS):
            term = column[a : a + height] * depth_kernel[a, e]
            mixed = term if mixed is None else mixed + term
    return mixed


def layer_apply(padded, depth_kernel, gain, up_matrix, down_matrix):
    height = padded.shape[0] - (KS - 1)
    width = padded.shape[1] - (KS - 1)
    spare = -width % 8
    widened = padded.astype(jnp.float32)
    if spare:
        widened = jnp.pad(widened, ((0, 0), (0, spare), (0, 0)))
    mixed = depthwise(widened, depth_kernel, height, width + spare)
    centered = mixed - jnp.mean(mixed, axis=-1, keepdims=True)
    variance = jnp.mean(centered * centered, axis=-1, keepdims=True)
    normed = (centered * lax.rsqrt(variance + 1e-06) * gain).astype(jnp.bfloat16)
    flat_cells = normed.reshape(height * (width + spare), -1)
    hidden = jax.nn.gelu(jnp.dot(flat_cells, up_matrix, preferred_element_type=jnp.float32)).astype(
        jnp.bfloat16
    )
    output = jnp.dot(hidden, down_matrix, preferred_element_type=jnp.float32).reshape(
        height, width + spare, -1
    )
    residual_part = widened[HALO : HALO + height, HALO : HALO + width + spare]
    return (residual_part + output).astype(jnp.bfloat16)[:, :width]


def per_device(
    swath_input,
    conv_weight,
    conv_bias,
    block_band,
    row_offset,
    col_offset,
    row_weights,
    col_weights,
    background,
    depth_weight,
    norm_gain,
    up_weight,
    down_weight,
):
    blocks_here = swath_input.shape[0]
    tile_rows = background.shape[0]
    tile_cols = background.shape[1]
    channels = background.shape[2]
    bands = lax.axis_size("lat")
    resampled = conv_resample(swath_input, conv_weight, conv_bias, row_weights, col_weights)
    own_band = lax.axis_index("lat")
    own_bands = block_band[:, 0]
    lane = jnp.arange(channels, dtype=jnp.int32)[None, :]
    header = jnp.where(
        lane == 0,
        row_offset[:, None],
        jnp.where(lane == 1, col_offset[:, None], jnp.where(lane == 2, own_bands[:, None], 0)),
    ).astype(jnp.bfloat16)
    header = jnp.broadcast_to(header[:, None, None, :], (blocks_here, 1, RW, channels))
    payload = jnp.concatenate([resampled, header], axis=1)
    block_list, row_list, col_list, band_list = [resampled], [row_offset], [col_offset], [own_bands]
    for step in (1, -1):
        got = shifted(payload, "lat", step)
        got_header = got[:, RB, 0, :].astype(jnp.int32)
        block_list.append(got[:, :RB])
        row_list.append(got_header[:, 0])
        col_list.append(got_header[:, 1])
        band_list.append(got_header[:, 2])
    arrived = jnp.concatenate(block_list, axis=0)
    all_rows = (jnp.concatenate(band_list, axis=0) - own_band) * tile_rows + jnp.concatenate(
        row_list, axis=0
    )
    all_cols = jnp.concatenate(col_list, axis=0)
    row_place = (
        jnp.arange(tile_rows, dtype=jnp.int32)[None, :, None]
        == all_rows[:, None, None] + jnp.arange(RB, dtype=jnp.int32)[None, None, :]
    ).astype(jnp.bfloat16)
    col_place = (
        jnp.arange(tile_cols, dtype=jnp.int32)[None, :, None]
        == all_cols[:, None, None] + jnp.arange(RW, dtype=jnp.int32)[None, None, :]
    ).astype(jnp.bfloat16)
    lifted = jnp.einsum(
        "shr,sruc->shuc", row_place, arrived, preferred_element_type=jnp.float32
    ).astype(jnp.bfloat16)
    summed = jnp.einsum("swu,shuc->hwc", col_place, lifted, preferred_element_type=jnp.float32)
    state = (background.astype(jnp.float32) + summed).astype(jnp.bfloat16)
    reach = HALO * LAYERS
    lon_wide = with_halo(state, (("lon", 1),), reach, True)
    size, length = lax.axis_size("lat"), lon_wide.shape[0]
    up = [(i, i + 1) for i in range(size - 1)]
    down = [(j, i) for i, j in up]
    north = lax.ppermute(lon_wide[length - reach :], "lat", up)
    south = lax.ppermute(lon_wide[:reach], "lat", down)
    first = (
        depth_weight[0],
        norm_gain[0],
        up_weight[0],
        down_weight[0],
    )
    middle = layer_apply(lon_wide, *first)
    top = layer_apply(jnp.concatenate([north, lon_wide[:reach]], axis=0), *first)
    bottom = layer_apply(jnp.concatenate([lon_wide[length - reach :], south], axis=0), *first)
    widened = jnp.concatenate([top, middle, bottom], axis=0)
    first_row = own_band * tile_rows
    margin = (widened.shape[0] - tile_rows) // 2
    grid_row = first_row - margin + jnp.arange(widened.shape[0], dtype=jnp.int32)
    inside = (grid_row >= 0) & (grid_row < bands * tile_rows)
    widened = jnp.where(inside[:, None, None], widened, jnp.zeros_like(widened))
    for layer_index in range(1, LAYERS):
        widened = layer_apply(
            widened,
            depth_weight[layer_index],
            norm_gain[layer_index],
            up_weight[layer_index],
            down_weight[layer_index],
        )
    return widened


def solution(mesh):
    in_specs = (
        P(("lat", "lon"), None, None, None),
        P(),
        P(),
        P(("lat", "lon"), None),
        P(("lat", "lon")),
        P(("lat", "lon")),
        P(("lat", "lon"), None, None),
        P(("lat", "lon"), None, None),
        P("lat", "lon", None),
        P(),
        P(),
        P(),
        P(),
    )
    out_specs = P("lat", "lon", None)
    return jax.shard_map(
        per_device, mesh=mesh, in_specs=in_specs, out_specs=out_specs, check_vma=False
    )
```

```python
import jax
import jax.numpy as jnp
from jax import lax
from jax.experimental import pallas as pl
from jax.experimental.pallas import tpu as pltpu
from jax.sharding import PartitionSpec as P

KS = 7
HALO = 3
LAYERS = 2
CAP = 2
RB = 16
RW = 16


def _expand(count, size, by_block, across=False):
    shape = (size, count) if across else (count, size)
    rows = lax.broadcasted_iota(jnp.int32, shape, 1 if across else 0)
    cols = lax.broadcasted_iota(jnp.int32, shape, 0 if across else 1)
    group = count // size if by_block else 1
    picked = rows // group if by_block else rows % size
    return (picked == cols).astype(jnp.bfloat16)


def _conv_body(x_ref, w_ref, b_ref, r_ref, c_ref, h_ref, o_ref, wide_ref):
    oh, ow, ch = x_ref.shape[1] // 2, x_ref.shape[2] // 2, o_ref.shape[2]
    cin = x_ref.shape[3]
    lanes = wide_ref.shape[3]
    parts = wide_ref.shape[0]
    for part in range(parts):
        wide_ref[part] = x_ref[0, :, :, part * lanes : (part + 1) * lanes].astype(jnp.float32)

    def parity(rp, cp):
        halves = [
            wide_ref[part, pl.ds(rp, oh, stride=2), pl.ds(cp, ow, stride=2), :].astype(x_ref.dtype)
            for part in range(parts)
        ]
        v = jnp.concatenate(halves, axis=-1)
        return v.reshape(oh * ow, cin)

    def tap(v, a, e):
        return jnp.dot(v, w_ref[a, e], preferred_element_type=jnp.float32)

    even_even, even_odd = parity(0, 0), parity(0, 1)
    odd_even, odd_odd = parity(1, 0), parity(1, 1)
    plain = tap(even_even, 1, 1) + tap(even_odd, 1, 2) + tap(odd_even, 2, 1) + tap(odd_odd, 2, 2)
    row_shift = tap(odd_even, 0, 1) + tap(odd_odd, 0, 2)
    col_shift = tap(even_odd, 1, 0) + tap(odd_odd, 2, 0)
    both_shift = tap(odd_odd, 0, 0)
    plain = plain.reshape(oh, ow, ch)
    row_shift = row_shift.reshape(oh, ow, ch)
    col_shift = col_shift.reshape(oh, ow, ch)
    both_shift = both_shift.reshape(oh, ow, ch)
    zero_row = jnp.zeros((1, ow, ch), jnp.float32)
    col_part = col_shift + jnp.concatenate([zero_row, both_shift[:-1]], axis=0)
    total = plain + jnp.concatenate([zero_row, row_shift[:-1]], axis=0)
    rolled = pltpu.roll(col_part, 1, 1)
    first_col = lax.broadcasted_iota(jnp.int32, (oh, ow, ch), 1) == 0
    total = total + jnp.where(first_col, 0.0, rolled)
    total = total + b_ref[...]
    features = jax.nn.gelu(total).astype(x_ref.dtype).reshape(oh * ow, ch)
    row_mix, col_mix = r_ref[0], c_ref[0]
    rb, rw = row_mix.shape[0], col_mix.shape[0]
    cells = rb * rw
    by_row = jnp.dot(_expand(cells, rb, True), row_mix, preferred_element_type=jnp.float32)
    by_col = jnp.dot(_expand(cells, rw, False), col_mix, preferred_element_type=jnp.float32)
    spread_row = jnp.dot(
        by_row.astype(x_ref.dtype), _expand(oh * ow, oh, True, True), preferred_element_type=jnp.float32
    )
    spread_col = jnp.dot(
        by_col.astype(x_ref.dtype), _expand(oh * ow, ow, False, True), preferred_element_type=jnp.float32
    )
    both = spread_row * spread_col
    high = both.astype(x_ref.dtype)
    low = (both - high.astype(jnp.float32)).astype(x_ref.dtype)
    mixed = jnp.dot(high, features, preferred_element_type=jnp.float32) + jnp.dot(
        low, features, preferred_element_type=jnp.float32
    )
    o_ref[0, :cells] = mixed.astype(o_ref.dtype)
    o_ref[0, cells:] = jnp.broadcast_to(h_ref[0], (o_ref.shape[1] - cells, ch))


def conv_resample(x, w, b, row_mix, col_mix, header):
    n, h, wd, cin = x.shape
    cout = w.shape[3]
    oh, ow = h // 2, wd // 2
    rb, rw = row_mix.shape[1], col_mix.shape[1]
    out = pl.pallas_call(
        _conv_body,
        grid=(n,),
        in_specs=[
            pl.BlockSpec((1, h, wd, cin), lambda i: (i, 0, 0, 0)),
            pl.BlockSpec((3, 3, cin, cout), lambda i: (0, 0, 0, 0)),
            pl.BlockSpec((1, cout), lambda i: (0, 0)),
            pl.BlockSpec((1, rb, oh), lambda i: (i, 0, 0)),
            pl.BlockSpec((1, rw, ow), lambda i: (i, 0, 0)),
            pl.BlockSpec((1, 1, cout), lambda i: (i, 0, 0)),
        ],
        out_specs=pl.BlockSpec((1, (rb + 1) * rw, cout), lambda i: (i, 0, 0)),
        out_shape=jax.ShapeDtypeStruct((n, (rb + 1) * rw, cout), jnp.bfloat16),
        scratch_shapes=[pltpu.VMEM((cin // 128, h, wd, 128), jnp.float32)],
        compiler_params=pltpu.CompilerParams(dimension_semantics=("arbitrary",)),
    )(x, w, b.reshape(1, cout), row_mix, col_mix, header)
    return out.reshape(n, rb + 1, rw, cout)


def shifted(value, axis, steps):
    count = lax.axis_size(axis)
    leading, last = (max(0, -steps), min(count, count - steps))
    return lax.ppermute(value, axis, [(source, source + steps) for source in range(leading, last)])


def with_halo(value, sides, width, wrap):
    for axis, dim in sides:
        size, length = (lax.axis_size(axis), value.shape[dim])
        up = [(i, (i + 1) % size) for i in range(size if wrap else size - 1)]
        down = [(j, i) for i, j in up]
        last = lax.slice_in_dim(value, length - width, length, axis=dim)
        leading = lax.slice_in_dim(value, 0, width, axis=dim)
        before = lax.ppermute(last, axis, up)
        after = lax.ppermute(leading, axis, down)
        value = jnp.concatenate([before, value, after], axis=dim)
    return value


def place_rows(onehot, values):
    flat_values = values.reshape(values.shape[0], -1)
    placed = jnp.dot(onehot.astype(values.dtype), flat_values, preferred_element_type=jnp.float32)
    return placed.astype(values.dtype).reshape((onehot.shape[0],) + values.shape[1:])


def place_ints(onehot, values):
    return jnp.sum(jnp.where(onehot, values[None, :], 0), axis=1)


def keep_local(keep, values):
    shaped = keep.reshape((keep.shape[0],) + (1,) * (values.ndim - 1))
    return jnp.where(shaped, values, jnp.zeros_like(values))


def depthwise(widened, depth_kernel, height, width):
    mixed = None
    for e in range(KS):
        column = widened[:, e : e + width]
        for a in range(KS):
            term = column[a : a + height] * depth_kernel[a, e]
            mixed = term if mixed is None else mixed + term
    return mixed


def layer_apply(padded, depth_kernel, gain, up_matrix, down_matrix):
    height = padded.shape[0] - (KS - 1)
    width = padded.shape[1] - (KS - 1)
    spare = -width % 8
    widened = padded.astype(jnp.float32)
    if spare:
        widened = jnp.pad(widened, ((0, 0), (0, spare), (0, 0)))
    mixed = depthwise(widened, depth_kernel, height, width + spare)
    centered = mixed - jnp.mean(mixed, axis=-1, keepdims=True)
    variance = jnp.mean(centered * centered, axis=-1, keepdims=True)
    normed = (centered * lax.rsqrt(variance + 1e-06) * gain).astype(jnp.bfloat16)
    flat_cells = normed.reshape(height * (width + spare), -1)
    hidden = jax.nn.gelu(jnp.dot(flat_cells, up_matrix, preferred_element_type=jnp.float32)).astype(
        jnp.bfloat16
    )
    output = jnp.dot(hidden, down_matrix, preferred_element_type=jnp.float32).reshape(
        height, width + spare, -1
    )
    residual_part = widened[HALO : HALO + height, HALO : HALO + width + spare]
    return (residual_part + output).astype(jnp.bfloat16)[:, :width]


def per_device(
    swath_input,
    conv_weight,
    conv_bias,
    block_band,
    row_offset,
    col_offset,
    row_weights,
    col_weights,
    background,
    depth_weight,
    norm_gain,
    up_weight,
    down_weight,
):
    blocks_here = swath_input.shape[0]
    tile_rows = background.shape[0]
    tile_cols = background.shape[1]
    channels = background.shape[2]
    bands = lax.axis_size("lat")
    own_band = lax.axis_index("lat")
    own_bands = block_band[:, 0]
    lane = jnp.arange(channels, dtype=jnp.int32)[None, :]
    header = jnp.where(
        lane == 0,
        row_offset[:, None],
        jnp.where(lane == 1, col_offset[:, None], jnp.where(lane == 2, own_bands[:, None], 0)),
    ).astype(jnp.bfloat16)
    payload = conv_resample(
        swath_input, conv_weight, conv_bias, row_weights, col_weights, header[:, None, :]
    )
    resampled = payload[:, :RB]
    block_list, row_list, col_list, band_list = [resampled], [row_offset], [col_offset], [own_bands]
    for step in (1, -1):
        got = shifted(payload, "lat", step)
        got_header = got[:, RB, 0, :].astype(jnp.int32)
        block_list.append(got[:, :RB])
        row_list.append(got_header[:, 0])
        col_list.append(got_header[:, 1])
        band_list.append(got_header[:, 2])
    arrived = jnp.concatenate(block_list, axis=0)
    all_rows = (jnp.concatenate(band_list, axis=0) - own_band) * tile_rows + jnp.concatenate(
        row_list, axis=0
    )
    all_cols = jnp.concatenate(col_list, axis=0)
    row_place = (
        jnp.arange(tile_rows, dtype=jnp.int32)[None, :, None]
        == all_rows[:, None, None] + jnp.arange(RB, dtype=jnp.int32)[None, None, :]
    ).astype(jnp.bfloat16)
    col_place = (
        jnp.arange(tile_cols, dtype=jnp.int32)[None, :, None]
        == all_cols[:, None, None] + jnp.arange(RW, dtype=jnp.int32)[None, None, :]
    ).astype(jnp.bfloat16)
    lifted = jnp.einsum(
        "shr,sruc->shuc", row_place, arrived, preferred_element_type=jnp.float32
    ).astype(jnp.bfloat16)
    summed = jnp.einsum("swu,shuc->hwc", col_place, lifted, preferred_element_type=jnp.float32)
    state = (background.astype(jnp.float32) + summed).astype(jnp.bfloat16)
    reach = HALO * LAYERS
    lon_wide = with_halo(state, (("lon", 1),), reach, True)
    size, length = lax.axis_size("lat"), lon_wide.shape[0]
    up = [(i, i + 1) for i in range(size - 1)]
    down = [(j, i) for i, j in up]
    north = lax.ppermute(lon_wide[length - reach :], "lat", up)
    south = lax.ppermute(lon_wide[:reach], "lat", down)
    first = (
        depth_weight[0],
        norm_gain[0],
        up_weight[0],
        down_weight[0],
    )
    middle = layer_apply(lon_wide, *first)
    top = layer_apply(jnp.concatenate([north, lon_wide[:reach]], axis=0), *first)
    bottom = layer_apply(jnp.concatenate([lon_wide[length - reach :], south], axis=0), *first)
    widened = jnp.concatenate([top, middle, bottom], axis=0)
    first_row = own_band * tile_rows
    margin = (widened.shape[0] - tile_rows) // 2
    grid_row = first_row - margin + jnp.arange(widened.shape[0], dtype=jnp.int32)
    inside = (grid_row >= 0) & (grid_row < bands * tile_rows)
    widened = jnp.where(inside[:, None, None], widened, jnp.zeros_like(widened))
    for layer_index in range(1, LAYERS):
        widened = layer_apply(
            widened,
            depth_weight[layer_index],
            norm_gain[layer_index],
            up_weight[layer_index],
            down_weight[layer_index],
        )
    return widened


def solution(mesh):
    in_specs = (
        P(("lat", "lon"), None, None, None),
        P(),
        P(),
        P(("lat", "lon"), None),
        P(("lat", "lon")),
        P(("lat", "lon")),
        P(("lat", "lon"), None, None),
        P(("lat", "lon"), None, None),
        P("lat", "lon", None),
        P(),
        P(),
        P(),
        P(),
    )
    out_specs = P("lat", "lon", None)
    return jax.shard_map(
        per_device, mesh=mesh, in_specs=in_specs, out_specs=out_specs, check_vma=False
    )
```

```python
import jax
import jax.numpy as jnp
from jax import lax
from jax.experimental import pallas as pl
from jax.experimental.pallas import tpu as pltpu
from jax.sharding import PartitionSpec as P

KS = 7
HALO = 3
LAYERS = 2
CAP = 2
RB = 16
RW = 16


def _expand(count, size, by_block, across=False):
    shape = (size, count) if across else (count, size)
    rows = lax.broadcasted_iota(jnp.int32, shape, 1 if across else 0)
    cols = lax.broadcasted_iota(jnp.int32, shape, 0 if across else 1)
    group = count // size if by_block else 1
    picked = rows // group if by_block else rows % size
    return (picked == cols).astype(jnp.bfloat16)


def _conv_body(x_ref, w_ref, b_ref, r_ref, c_ref, o_ref, wide_ref):
    oh, ow, ch = x_ref.shape[1] // 2, x_ref.shape[2] // 2, o_ref.shape[2]
    cin = x_ref.shape[3]
    lanes = wide_ref.shape[3]
    parts = wide_ref.shape[0]
    for part in range(parts):
        wide_ref[part] = x_ref[0, :, :, part * lanes : (part + 1) * lanes].astype(jnp.float32)

    def parity(rp, cp):
        halves = [
            wide_ref[part, pl.ds(rp, oh, stride=2), pl.ds(cp, ow, stride=2), :].astype(x_ref.dtype)
            for part in range(parts)
        ]
        v = jnp.concatenate(halves, axis=-1)
        return v.reshape(oh * ow, cin)

    def tap(v, a, e):
        return jnp.dot(v, w_ref[a, e], preferred_element_type=jnp.float32)

    even_even, even_odd = parity(0, 0), parity(0, 1)
    odd_even, odd_odd = parity(1, 0), parity(1, 1)
    plain = tap(even_even, 1, 1) + tap(even_odd, 1, 2) + tap(odd_even, 2, 1) + tap(odd_odd, 2, 2)
    row_shift = tap(odd_even, 0, 1) + tap(odd_odd, 0, 2)
    col_shift = tap(even_odd, 1, 0) + tap(odd_odd, 2, 0)
    both_shift = tap(odd_odd, 0, 0)
    plain = plain.reshape(oh, ow, ch)
    row_shift = row_shift.reshape(oh, ow, ch)
    col_shift = col_shift.reshape(oh, ow, ch)
    both_shift = both_shift.reshape(oh, ow, ch)
    zero_row = jnp.zeros((1, ow, ch), jnp.float32)
    col_part = col_shift + jnp.concatenate([zero_row, both_shift[:-1]], axis=0)
    total = plain + jnp.concatenate([zero_row, row_shift[:-1]], axis=0)
    rolled = pltpu.roll(col_part, 1, 1)
    first_col = lax.broadcasted_iota(jnp.int32, (oh, ow, ch), 1) == 0
    total = total + jnp.where(first_col, 0.0, rolled)
    total = total + b_ref[...]
    features = jax.nn.gelu(total).astype(x_ref.dtype).reshape(oh * ow, ch)
    row_mix, col_mix = r_ref[0], c_ref[0]
    rb, rw = row_mix.shape[0], col_mix.shape[0]
    cells = rb * rw
    by_row = jnp.dot(_expand(cells, rb, True), row_mix, preferred_element_type=jnp.float32)
    by_col = jnp.dot(_expand(cells, rw, False), col_mix, preferred_element_type=jnp.float32)
    spread_row = jnp.dot(
        by_row.astype(x_ref.dtype), _expand(oh * ow, oh, True, True), preferred_element_type=jnp.float32
    )
    spread_col = jnp.dot(
        by_col.astype(x_ref.dtype), _expand(oh * ow, ow, False, True), preferred_element_type=jnp.float32
    )
    both = spread_row * spread_col
    high = both.astype(x_ref.dtype)
    low = (both - high.astype(jnp.float32)).astype(x_ref.dtype)
    mixed = jnp.dot(high, features, preferred_element_type=jnp.float32) + jnp.dot(
        low, features, preferred_element_type=jnp.float32
    )
    o_ref[0, :cells] = mixed.astype(o_ref.dtype)
    o_ref[0, cells:] = jnp.zeros((o_ref.shape[1] - cells, ch), o_ref.dtype)


def conv_resample(x, w, b, row_mix, col_mix):
    n, h, wd, cin = x.shape
    cout = w.shape[3]
    oh, ow = h // 2, wd // 2
    rb, rw = row_mix.shape[1], col_mix.shape[1]
    out = pl.pallas_call(
        _conv_body,
        grid=(n,),
        in_specs=[
            pl.BlockSpec((1, h, wd, cin), lambda i: (i, 0, 0, 0)),
            pl.BlockSpec((3, 3, cin, cout), lambda i: (0, 0, 0, 0)),
            pl.BlockSpec((1, cout), lambda i: (0, 0)),
            pl.BlockSpec((1, rb, oh), lambda i: (i, 0, 0)),
            pl.BlockSpec((1, rw, ow), lambda i: (i, 0, 0)),
        ],
        out_specs=pl.BlockSpec((1, (rb + 1) * rw, cout), lambda i: (i, 0, 0)),
        out_shape=jax.ShapeDtypeStruct((n, (rb + 1) * rw, cout), jnp.bfloat16),
        scratch_shapes=[pltpu.VMEM((cin // 128, h, wd, 128), jnp.float32)],
        compiler_params=pltpu.CompilerParams(dimension_semantics=("arbitrary",)),
    )(x, w, b.reshape(1, cout), row_mix, col_mix)
    return out.reshape(n, rb + 1, rw, cout)


def shifted(value, axis, steps):
    count = lax.axis_size(axis)
    leading, last = (max(0, -steps), min(count, count - steps))
    return lax.ppermute(value, axis, [(source, source + steps) for source in range(leading, last)])


def with_halo(value, sides, width, wrap):
    for axis, dim in sides:
        size, length = (lax.axis_size(axis), value.shape[dim])
        up = [(i, (i + 1) % size) for i in range(size if wrap else size - 1)]
        down = [(j, i) for i, j in up]
        last = lax.slice_in_dim(value, length - width, length, axis=dim)
        leading = lax.slice_in_dim(value, 0, width, axis=dim)
        before = lax.ppermute(last, axis, up)
        after = lax.ppermute(leading, axis, down)
        value = jnp.concatenate([before, value, after], axis=dim)
    return value


def place_rows(onehot, values):
    flat_values = values.reshape(values.shape[0], -1)
    placed = jnp.dot(onehot.astype(values.dtype), flat_values, preferred_element_type=jnp.float32)
    return placed.astype(values.dtype).reshape((onehot.shape[0],) + values.shape[1:])


def place_ints(onehot, values):
    return jnp.sum(jnp.where(onehot, values[None, :], 0), axis=1)


def keep_local(keep, values):
    shaped = keep.reshape((keep.shape[0],) + (1,) * (values.ndim - 1))
    return jnp.where(shaped, values, jnp.zeros_like(values))


def depthwise(widened, depth_kernel, height, width):
    mixed = None
    for e in range(KS):
        column = widened[:, e : e + width]
        for a in range(KS):
            term = column[a : a + height] * depth_kernel[a, e]
            mixed = term if mixed is None else mixed + term
    return mixed


def layer_apply(padded, depth_kernel, gain, up_matrix, down_matrix):
    height = padded.shape[0] - (KS - 1)
    width = padded.shape[1] - (KS - 1)
    spare = -width % 8
    widened = padded.astype(jnp.float32)
    if spare:
        widened = jnp.pad(widened, ((0, 0), (0, spare), (0, 0)))
    mixed = depthwise(widened, depth_kernel, height, width + spare)
    centered = mixed - jnp.mean(mixed, axis=-1, keepdims=True)
    variance = jnp.mean(centered * centered, axis=-1, keepdims=True)
    normed = (centered * lax.rsqrt(variance + 1e-06) * gain).astype(jnp.bfloat16)
    flat_cells = normed.reshape(height * (width + spare), -1)
    hidden = jax.nn.gelu(jnp.dot(flat_cells, up_matrix, preferred_element_type=jnp.float32)).astype(
        jnp.bfloat16
    )
    output = jnp.dot(hidden, down_matrix, preferred_element_type=jnp.float32).reshape(
        height, width + spare, -1
    )
    residual_part = widened[HALO : HALO + height, HALO : HALO + width + spare]
    return (residual_part + output).astype(jnp.bfloat16)[:, :width]


def per_device(
    swath_input,
    conv_weight,
    conv_bias,
    block_band,
    row_offset,
    col_offset,
    row_weights,
    col_weights,
    background,
    depth_weight,
    norm_gain,
    up_weight,
    down_weight,
):
    blocks_here = swath_input.shape[0]
    tile_rows = background.shape[0]
    tile_cols = background.shape[1]
    channels = background.shape[2]
    bands = lax.axis_size("lat")
    resampled = conv_resample(swath_input, conv_weight, conv_bias, row_weights, col_weights)
    own_band = lax.axis_index("lat")
    own_bands = block_band[:, 0]
    lane = jnp.arange(channels, dtype=jnp.int32)[None, :]
    header = jnp.where(
        lane == 0,
        row_offset[:, None],
        jnp.where(lane == 1, col_offset[:, None], jnp.where(lane == 2, own_bands[:, None], 0)),
    ).astype(jnp.bfloat16)
    payload = resampled.at[:, RB, 0, :].set(header)
    block_list, row_list, col_list, band_list = [payload], [row_offset], [col_offset], [own_bands]
    for step in (1, -1):
        got = shifted(payload, "lat", step)
        got_header = got[:, RB, 0, :].astype(jnp.int32)
        block_list.append(got)
        row_list.append(got_header[:, 0])
        col_list.append(got_header[:, 1])
        band_list.append(got_header[:, 2])
    arrived = jnp.concatenate(block_list, axis=0)
    all_rows = (jnp.concatenate(band_list, axis=0) - own_band) * tile_rows + jnp.concatenate(
        row_list, axis=0
    )
    all_cols = jnp.concatenate(col_list, axis=0)
    row_place = (
        jnp.arange(tile_rows, dtype=jnp.int32)[None, :, None]
        == all_rows[:, None, None] + jnp.arange(RB + 1, dtype=jnp.int32)[None, None, :]
    ) & (jnp.arange(RB + 1, dtype=jnp.int32) < RB)[None, None, :]
    row_place = row_place.astype(jnp.bfloat16)
    col_place = (
        jnp.arange(tile_cols, dtype=jnp.int32)[None, :, None]
        == all_cols[:, None, None] + jnp.arange(RW, dtype=jnp.int32)[None, None, :]
    ).astype(jnp.bfloat16)
    lifted = jnp.einsum(
        "shr,sruc->shuc", row_place, arrived, preferred_element_type=jnp.float32
    ).astype(jnp.bfloat16)
    summed = jnp.einsum("swu,shuc->hwc", col_place, lifted, preferred_element_type=jnp.float32)
    state = (background.astype(jnp.float32) + summed).astype(jnp.bfloat16)
    reach = HALO * LAYERS
    lon_wide = with_halo(state, (("lon", 1),), reach, True)
    size, length = lax.axis_size("lat"), lon_wide.shape[0]
    up = [(i, i + 1) for i in range(size - 1)]
    down = [(j, i) for i, j in up]
    north = lax.ppermute(lon_wide[length - reach :], "lat", up)
    south = lax.ppermute(lon_wide[:reach], "lat", down)
    first = (
        depth_weight[0],
        norm_gain[0],
        up_weight[0],
        down_weight[0],
    )
    middle = layer_apply(lon_wide, *first)
    top = layer_apply(jnp.concatenate([north, lon_wide[:reach]], axis=0), *first)
    bottom = layer_apply(jnp.concatenate([lon_wide[length - reach :], south], axis=0), *first)
    widened = jnp.concatenate([top, middle, bottom], axis=0)
    first_row = own_band * tile_rows
    margin = (widened.shape[0] - tile_rows) // 2
    grid_row = first_row - margin + jnp.arange(widened.shape[0], dtype=jnp.int32)
    inside = (grid_row >= 0) & (grid_row < bands * tile_rows)
    widened = jnp.where(inside[:, None, None], widened, jnp.zeros_like(widened))
    for layer_index in range(1, LAYERS):
        widened = layer_apply(
            widened,
            depth_weight[layer_index],
            norm_gain[layer_index],
            up_weight[layer_index],
            down_weight[layer_index],
        )
    return widened


def solution(mesh):
    in_specs = (
        P(("lat", "lon"), None, None, None),
        P(),
        P(),
        P(("lat", "lon"), None),
        P(("lat", "lon")),
        P(("lat", "lon")),
        P(("lat", "lon"), None, None),
        P(("lat", "lon"), None, None),
        P("lat", "lon", None),
        P(),
        P(),
        P(),
        P(),
    )
    out_specs = P("lat", "lon", None)
    return jax.shard_map(
        per_device, mesh=mesh, in_specs=in_specs, out_specs=out_specs, check_vma=False
    )
```

```python
import jax
import jax.numpy as jnp
from jax import lax
from jax.experimental import pallas as pl
from jax.experimental.pallas import tpu as pltpu
from jax.sharding import PartitionSpec as P

KS = 7
HALO = 3
LAYERS = 2
CAP = 2
RB = 16
RW = 16


def _expand(count, size, by_block, across=False):
    shape = (size, count) if across else (count, size)
    rows = lax.broadcasted_iota(jnp.int32, shape, 1 if across else 0)
    cols = lax.broadcasted_iota(jnp.int32, shape, 0 if across else 1)
    group = count // size if by_block else 1
    picked = rows // group if by_block else rows % size
    return (picked == cols).astype(jnp.bfloat16)


def _conv_body(s_ref, x_ref, w_ref, b_ref, r_ref, c_ref, o_ref, wide_ref):
    oh, ow, ch = x_ref.shape[1] // 2, x_ref.shape[2] // 2, o_ref.shape[2]
    cin = x_ref.shape[3]
    lanes = wide_ref.shape[3]
    parts = wide_ref.shape[0]
    for part in range(parts):
        wide_ref[part] = x_ref[0, :, :, part * lanes : (part + 1) * lanes].astype(jnp.float32)

    def parity(rp, cp):
        halves = [
            wide_ref[part, pl.ds(rp, oh, stride=2), pl.ds(cp, ow, stride=2), :].astype(x_ref.dtype)
            for part in range(parts)
        ]
        v = jnp.concatenate(halves, axis=-1)
        return v.reshape(oh * ow, cin)

    def tap(v, a, e):
        return jnp.dot(v, w_ref[a, e], preferred_element_type=jnp.float32)

    even_even, even_odd = parity(0, 0), parity(0, 1)
    odd_even, odd_odd = parity(1, 0), parity(1, 1)
    plain = tap(even_even, 1, 1) + tap(even_odd, 1, 2) + tap(odd_even, 2, 1) + tap(odd_odd, 2, 2)
    row_shift = tap(odd_even, 0, 1) + tap(odd_odd, 0, 2)
    col_shift = tap(even_odd, 1, 0) + tap(odd_odd, 2, 0)
    both_shift = tap(odd_odd, 0, 0)
    plain = plain.reshape(oh, ow, ch)
    row_shift = row_shift.reshape(oh, ow, ch)
    col_shift = col_shift.reshape(oh, ow, ch)
    both_shift = both_shift.reshape(oh, ow, ch)
    zero_row = jnp.zeros((1, ow, ch), jnp.float32)
    col_part = col_shift + jnp.concatenate([zero_row, both_shift[:-1]], axis=0)
    total = plain + jnp.concatenate([zero_row, row_shift[:-1]], axis=0)
    rolled = pltpu.roll(col_part, 1, 1)
    first_col = lax.broadcasted_iota(jnp.int32, (oh, ow, ch), 1) == 0
    total = total + jnp.where(first_col, 0.0, rolled)
    total = total + b_ref[...]
    features = jax.nn.gelu(total).astype(x_ref.dtype).reshape(oh * ow, ch)
    row_mix, col_mix = r_ref[0], c_ref[0]
    rb, rw = row_mix.shape[0], col_mix.shape[0]
    cells = rb * rw
    by_row = jnp.dot(_expand(cells, rb, True), row_mix, preferred_element_type=jnp.float32)
    by_col = jnp.dot(_expand(cells, rw, False), col_mix, preferred_element_type=jnp.float32)
    spread_row = jnp.dot(
        by_row.astype(x_ref.dtype), _expand(oh * ow, oh, True, True), preferred_element_type=jnp.float32
    )
    spread_col = jnp.dot(
        by_col.astype(x_ref.dtype), _expand(oh * ow, ow, False, True), preferred_element_type=jnp.float32
    )
    both = spread_row * spread_col
    high = both.astype(x_ref.dtype)
    low = (both - high.astype(jnp.float32)).astype(x_ref.dtype)
    mixed = jnp.dot(high, features, preferred_element_type=jnp.float32) + jnp.dot(
        low, features, preferred_element_type=jnp.float32
    )
    o_ref[0, :cells] = mixed.astype(o_ref.dtype)
    step = pl.program_id(0)
    lane = lax.broadcasted_iota(jnp.int32, (o_ref.shape[1] - cells, ch), 1)
    header = jnp.where(
        lane == 0,
        s_ref[3 * step],
        jnp.where(lane == 1, s_ref[3 * step + 1], jnp.where(lane == 2, s_ref[3 * step + 2], 0)),
    )
    o_ref[0, cells:] = header.astype(jnp.float32).astype(o_ref.dtype)


def conv_resample(x, w, b, row_mix, col_mix, table):
    n, h, wd, cin = x.shape
    cout = w.shape[3]
    oh, ow = h // 2, wd // 2
    rb, rw = row_mix.shape[1], col_mix.shape[1]
    out = pl.pallas_call(
        _conv_body,
        grid_spec=pltpu.PrefetchScalarGridSpec(
            num_scalar_prefetch=1,
            grid=(n,),
            in_specs=[
                pl.BlockSpec((1, h, wd, cin), lambda i, s: (i, 0, 0, 0)),
                pl.BlockSpec((3, 3, cin, cout), lambda i, s: (0, 0, 0, 0)),
                pl.BlockSpec((1, cout), lambda i, s: (0, 0)),
                pl.BlockSpec((1, rb, oh), lambda i, s: (i, 0, 0)),
                pl.BlockSpec((1, rw, ow), lambda i, s: (i, 0, 0)),
            ],
            out_specs=pl.BlockSpec((1, (rb + 1) * rw, cout), lambda i, s: (i, 0, 0)),
            scratch_shapes=[pltpu.VMEM((cin // 128, h, wd, 128), jnp.float32)],
        ),
        out_shape=jax.ShapeDtypeStruct((n, (rb + 1) * rw, cout), jnp.bfloat16),
        compiler_params=pltpu.CompilerParams(dimension_semantics=("arbitrary",)),
    )(table, x, w, b.reshape(1, cout), row_mix, col_mix)
    return out.reshape(n, rb + 1, rw, cout)


def shifted(value, axis, steps):
    count = lax.axis_size(axis)
    leading, last = (max(0, -steps), min(count, count - steps))
    return lax.ppermute(value, axis, [(source, source + steps) for source in range(leading, last)])


def with_halo(value, sides, width, wrap):
    for axis, dim in sides:
        size, length = (lax.axis_size(axis), value.shape[dim])
        up = [(i, (i + 1) % size) for i in range(size if wrap else size - 1)]
        down = [(j, i) for i, j in up]
        last = lax.slice_in_dim(value, length - width, length, axis=dim)
        leading = lax.slice_in_dim(value, 0, width, axis=dim)
        before = lax.ppermute(last, axis, up)
        after = lax.ppermute(leading, axis, down)
        value = jnp.concatenate([before, value, after], axis=dim)
    return value


def place_rows(onehot, values):
    flat_values = values.reshape(values.shape[0], -1)
    placed = jnp.dot(onehot.astype(values.dtype), flat_values, preferred_element_type=jnp.float32)
    return placed.astype(values.dtype).reshape((onehot.shape[0],) + values.shape[1:])


def place_ints(onehot, values):
    return jnp.sum(jnp.where(onehot, values[None, :], 0), axis=1)


def keep_local(keep, values):
    shaped = keep.reshape((keep.shape[0],) + (1,) * (values.ndim - 1))
    return jnp.where(shaped, values, jnp.zeros_like(values))


def depthwise(widened, depth_kernel, height, width):
    mixed = None
    for e in range(KS):
        column = widened[:, e : e + width]
        for a in range(KS):
            term = column[a : a + height] * depth_kernel[a, e]
            mixed = term if mixed is None else mixed + term
    return mixed


def layer_apply(padded, depth_kernel, gain, up_matrix, down_matrix):
    height = padded.shape[0] - (KS - 1)
    width = padded.shape[1] - (KS - 1)
    spare = -width % 8
    widened = padded.astype(jnp.float32)
    if spare:
        widened = jnp.pad(widened, ((0, 0), (0, spare), (0, 0)))
    mixed = depthwise(widened, depth_kernel, height, width + spare)
    centered = mixed - jnp.mean(mixed, axis=-1, keepdims=True)
    variance = jnp.mean(centered * centered, axis=-1, keepdims=True)
    normed = (centered * lax.rsqrt(variance + 1e-06) * gain).astype(jnp.bfloat16)
    flat_cells = normed.reshape(height * (width + spare), -1)
    hidden = jax.nn.gelu(jnp.dot(flat_cells, up_matrix, preferred_element_type=jnp.float32)).astype(
        jnp.bfloat16
    )
    output = jnp.dot(hidden, down_matrix, preferred_element_type=jnp.float32).reshape(
        height, width + spare, -1
    )
    residual_part = widened[HALO : HALO + height, HALO : HALO + width + spare]
    return (residual_part + output).astype(jnp.bfloat16)[:, :width]


def per_device(
    swath_input,
    conv_weight,
    conv_bias,
    block_band,
    row_offset,
    col_offset,
    row_weights,
    col_weights,
    background,
    depth_weight,
    norm_gain,
    up_weight,
    down_weight,
):
    blocks_here = swath_input.shape[0]
    tile_rows = background.shape[0]
    tile_cols = background.shape[1]
    channels = background.shape[2]
    bands = lax.axis_size("lat")
    own_band = lax.axis_index("lat")
    own_bands = block_band[:, 0]
    table = jnp.stack([row_offset, col_offset, own_bands], axis=1).reshape(-1).astype(jnp.int32)
    payload = conv_resample(swath_input, conv_weight, conv_bias, row_weights, col_weights, table)
    block_list, row_list, col_list, band_list = [payload], [row_offset], [col_offset], [own_bands]
    for step in (1, -1):
        got = shifted(payload, "lat", step)
        got_header = got[:, RB, 0, :].astype(jnp.int32)
        block_list.append(got)
        row_list.append(got_header[:, 0])
        col_list.append(got_header[:, 1])
        band_list.append(got_header[:, 2])
    arrived = jnp.concatenate(block_list, axis=0)
    all_rows = (jnp.concatenate(band_list, axis=0) - own_band) * tile_rows + jnp.concatenate(
        row_list, axis=0
    )
    all_cols = jnp.concatenate(col_list, axis=0)
    row_place = (
        jnp.arange(tile_rows, dtype=jnp.int32)[None, :, None]
        == all_rows[:, None, None] + jnp.arange(RB + 1, dtype=jnp.int32)[None, None, :]
    ) & (jnp.arange(RB + 1, dtype=jnp.int32) < RB)[None, None, :]
    row_place = row_place.astype(jnp.bfloat16)
    col_place = (
        jnp.arange(tile_cols, dtype=jnp.int32)[None, :, None]
        == all_cols[:, None, None] + jnp.arange(RW, dtype=jnp.int32)[None, None, :]
    ).astype(jnp.bfloat16)
    lifted = jnp.einsum(
        "shr,sruc->shuc", row_place, arrived, preferred_element_type=jnp.float32
    ).astype(jnp.bfloat16)
    summed = jnp.einsum("swu,shuc->hwc", col_place, lifted, preferred_element_type=jnp.float32)
    state = (background.astype(jnp.float32) + summed).astype(jnp.bfloat16)
    reach = HALO * LAYERS
    lon_wide = with_halo(state, (("lon", 1),), reach, True)
    size, length = lax.axis_size("lat"), lon_wide.shape[0]
    up = [(i, i + 1) for i in range(size - 1)]
    down = [(j, i) for i, j in up]
    north = lax.ppermute(lon_wide[length - reach :], "lat", up)
    south = lax.ppermute(lon_wide[:reach], "lat", down)
    first = (
        depth_weight[0],
        norm_gain[0],
        up_weight[0],
        down_weight[0],
    )
    middle = layer_apply(lon_wide, *first)
    top = layer_apply(jnp.concatenate([north, lon_wide[:reach]], axis=0), *first)
    bottom = layer_apply(jnp.concatenate([lon_wide[length - reach :], south], axis=0), *first)
    widened = jnp.concatenate([top, middle, bottom], axis=0)
    first_row = own_band * tile_rows
    margin = (widened.shape[0] - tile_rows) // 2
    grid_row = first_row - margin + jnp.arange(widened.shape[0], dtype=jnp.int32)
    inside = (grid_row >= 0) & (grid_row < bands * tile_rows)
    widened = jnp.where(inside[:, None, None], widened, jnp.zeros_like(widened))
    for layer_index in range(1, LAYERS):
        widened = layer_apply(
            widened,
            depth_weight[layer_index],
            norm_gain[layer_index],
            up_weight[layer_index],
            down_weight[layer_index],
        )
    return widened


def solution(mesh):
    in_specs = (
        P(("lat", "lon"), None, None, None),
        P(),
        P(),
        P(("lat", "lon"), None),
        P(("lat", "lon")),
        P(("lat", "lon")),
        P(("lat", "lon"), None, None),
        P(("lat", "lon"), None, None),
        P("lat", "lon", None),
        P(),
        P(),
        P(),
        P(),
    )
    out_specs = P("lat", "lon", None)
    return jax.shard_map(
        per_device, mesh=mesh, in_specs=in_specs, out_specs=out_specs, check_vma=False
    )
```
